32 devices in a mesh: chan: 4 (over y, x), tm: 8 (over z, core).
Axes of the slice: x: 2, y: 2, z: 4, core: 2. Of those that a mesh axis runs over, the one named last changes fastest.
Arguments:
- raw_samples: float32 [32, 512, 2048], P('tm', 'chan'), may hold values from -80 to 80
Outputs:
- correlations: float32 [512, 512, 256], P(('chan', 'tm'))
The draws below stay inside these ranges and needn't reach their ends.
All inputs are finite; a program needn't handle non-finite values.
Results may differ from the reference program's by a relative error of at most 0.0043.
Values may be sent and summed in bfloat16 or wider, within the bound.
No kernel may reach another device: no remote copies, remote signals or barrier semaphores. Data moves between devices by JAX's collectives and lax.ppermute only.
A program may use at most 192 MiB of HBM per device.

```python
import math
import jax
import jax.numpy as jnp
from jax import lax

CH = 512
NT = 1024
LAGS = 256
S_DEV = 4
F = 128
RAW = 2048
SEGS = 32
N_CHAN = 4
N_TM = 8


def draw_raw_samples(key, part):
    key_list = jax.random.split(jax.random.fold_in(key, 11), 5)
    full_shape = (SEGS, CH, RAW)
    noise_field = jnp.clip(jax.random.normal(key_list[0], full_shape, jnp.float32), -4.0, 4.0)
    row_scale = jnp.exp(jax.random.uniform(key_list[1], (SEGS, CH, 1), jnp.float32, 0.0, math.log(10.0)))
    tone_level = jnp.exp(jax.random.uniform(key_list[2], (SEGS, CH, 1), jnp.float32, math.log(0.3), math.log(3.0)))
    tone_rate = jax.random.uniform(key_list[3], (SEGS, CH, 1), jnp.float32, 0.005, 0.06)
    tone_phase = jax.random.uniform(key_list[4], (SEGS, CH, 1), jnp.float32, -math.pi, math.pi)
    sample_time = jnp.arange(RAW, dtype=jnp.float32)
    tone_wave = tone_level * jnp.sin(2.0 * math.pi * tone_rate * sample_time + tone_phase)
    return row_scale * (noise_field + tone_wave)


def setup_inputs(seed: int = 0) -> dict:
    keys = jax.random.split(jax.random.key(seed), 2)
    return {
        "raw_samples": draw_raw_samples(jax.random.fold_in(keys[1], 71), 0),
    }


def decimate(raw_samples):
    even_taps = raw_samples[..., 0::2]
    odd_taps = raw_samples[..., 1::2]
    odd_before = jnp.concatenate([jnp.zeros_like(odd_taps[..., :1]), odd_taps[..., :-1]], axis=-1)
    return 0.25 * odd_before + 0.5 * even_taps + 0.25 * odd_taps

def whiten(real_part, imag_part):
    power = real_part * real_part + imag_part * imag_part
    level = lax.optimization_barrier(jnp.mean(power, axis=-1, keepdims=True))
    factor = 1.0 / jnp.sqrt(power + 0.1 * level + 1e-06)
    return (real_part * factor, imag_part * factor)

def lag_table(freq_count, sample_count, lag_count):
    freq_index = jnp.arange(1, freq_count + 1, dtype=jnp.int32)
    lag_index = jnp.arange(lag_count, dtype=jnp.int32) - lag_count // 2
    turns = freq_index[:, None] * (lag_index[None, :] % sample_count) % sample_count
    angle = turns.astype(jnp.float32) * (2.0 * math.pi / sample_count)
    return jnp.concatenate([jnp.cos(angle), -jnp.sin(angle)], axis=0).astype(jnp.bfloat16)

def reference(raw_samples):
    signal = decimate(raw_samples)
    spectrum = jnp.fft.rfft(signal, axis=-1)[..., 1:F + 1]
    real_w, imag_w = whiten(jnp.real(spectrum), jnp.imag(spectrum))
    real_groups = real_w.reshape(N_TM, S_DEV, CH, F)
    imag_groups = imag_w.reshape(N_TM, S_DEV, CH, F)
    grouped = lax.optimization_barrier(jnp.concatenate([real_groups, imag_groups], axis=1).astype(jnp.bfloat16)).astype(jnp.float32)
    turned = lax.optimization_barrier(jnp.concatenate([imag_groups, -real_groups], axis=1).astype(jnp.bfloat16)).astype(jnp.float32)
    table = lag_table(F, NT, LAGS).astype(jnp.float32)
    norm_scale = 1.0 / math.sqrt(F * SEGS)
    row_width = CH // N_CHAN

    def one_block(row_start):
        left_part = lax.dynamic_slice_in_dim(grouped, row_start, row_width, axis=2)
        left_turned = lax.dynamic_slice_in_dim(turned, row_start, row_width, axis=2)

        def add_group(totals, members):
            left_group, turned_group, right_group = members
            real_cross = jnp.einsum('sik,sjk->ijk', left_group, right_group, precision=lax.Precision.HIGHEST)
            imag_cross = jnp.einsum('sik,sjk->ijk', turned_group, right_group, precision=lax.Precision.HIGHEST)
            real_cross = lax.optimization_barrier(real_cross.astype(jnp.bfloat16)).astype(jnp.float32)
            imag_cross = lax.optimization_barrier(imag_cross.astype(jnp.bfloat16)).astype(jnp.float32)
            return ((totals[0] + real_cross, totals[1] + imag_cross), None)
        zeros_init = jnp.zeros((row_width, CH, F), jnp.float32)
        sums, unused = lax.scan(add_group, (zeros_init, zeros_init), (left_part, left_turned, grouped))
        both_parts = jnp.concatenate([sums[0], sums[1]], axis=-1)
        return jnp.einsum('ijk,kl->ijl', both_parts, table, precision=lax.Precision.HIGHEST) * norm_scale
    block_starts = (jnp.arange(CH // row_width) * row_width).astype(jnp.int32)
    blocks = lax.map(one_block, block_starts)
    return blocks.reshape(CH, CH, LAGS)
```

```python
import math

import jax
import jax.numpy as jnp
from jax import lax
from jax.sharding import PartitionSpec as P

LAGS = 256


def decimate(raw_samples):
    even_taps = raw_samples[..., 0::2]
    odd_taps = raw_samples[..., 1::2]
    odd_before = jnp.concatenate([jnp.zeros_like(odd_taps[..., :1]), odd_taps[..., :-1]], axis=-1)
    return 0.25 * odd_before + 0.5 * even_taps + 0.25 * odd_taps


def whiten(real_part, imag_part):
    power = real_part * real_part + imag_part * imag_part
    level = jnp.mean(power, axis=-1, keepdims=True)
    factor = 1.0 / jnp.sqrt(power + 0.1 * level + 1e-06)
    return (real_part * factor, imag_part * factor)


def lag_table(freq_count, sample_count, lag_count):
    freq_index = jnp.arange(1, freq_count + 1, dtype=jnp.int32)
    lag_index = jnp.arange(lag_count, dtype=jnp.int32) - lag_count // 2
    turns = freq_index[:, None] * (lag_index[None, :] % sample_count) % sample_count
    angle = turns.astype(jnp.float32) * (2.0 * math.pi / sample_count)
    return jnp.concatenate([jnp.cos(angle), -jnp.sin(angle)], axis=0).astype(jnp.bfloat16)


def transform_tables(sample_count, freq_count):
    time_index = jnp.arange(sample_count, dtype=jnp.int32)
    freq_index = jnp.arange(1, freq_count + 1, dtype=jnp.int32)
    turns = time_index[:, None] * freq_index[None, :] % sample_count
    angle = turns.astype(jnp.float32) * (2.0 * math.pi / sample_count)
    return (jnp.cos(angle), -jnp.sin(angle))


def per_device(raw_samples):
    seg_count, block_width, raw_length = raw_samples.shape
    sample_count = raw_length // 2
    freq_count = sample_count // 8
    chan_count = lax.axis_size("chan")
    time_count = lax.axis_size("tm")
    channel_total = block_width * chan_count
    row_width = channel_total // (chan_count * time_count)
    signal = decimate(raw_samples).reshape(seg_count * block_width, sample_count)
    cos_table, sin_table = transform_tables(sample_count, freq_count)
    real_part = jnp.dot(
        signal, cos_table, precision=lax.Precision.HIGHEST, preferred_element_type=jnp.float32
    )
    imag_part = jnp.dot(
        signal, sin_table, precision=lax.Precision.HIGHEST, preferred_element_type=jnp.float32
    )
    real_part = real_part.reshape(seg_count, block_width, freq_count)
    imag_part = imag_part.reshape(seg_count, block_width, freq_count)
    real_w, imag_w = whiten(real_part, imag_part)
    local_spec = jnp.stack([real_w, imag_w], axis=0).astype(jnp.bfloat16)
    every = lax.all_gather(local_spec, ("chan", "tm"), axis=0)
    every = every.reshape(chan_count, time_count, 2, seg_count, block_width, freq_count)
    chan_index = lax.axis_index("chan")
    tm_index = lax.axis_index("tm")
    own_block = lax.dynamic_index_in_dim(every, chan_index, 0, keepdims=False)
    rows = lax.dynamic_slice_in_dim(own_block, tm_index * row_width, row_width, axis=3)
    turned = jnp.stack([rows[:, 1], -rows[:, 0]], axis=1)
    left = jnp.concatenate([rows, turned], axis=3)
    cross = jnp.einsum("trsak,ctrswk->kacw", left, every, preferred_element_type=jnp.float32)
    cross = cross.reshape(freq_count, 2, row_width, channel_total)
    table = lag_table(freq_count, sample_count, LAGS).reshape(2, freq_count, LAGS)
    high = cross.astype(jnp.bfloat16)
    low = (cross - high.astype(jnp.float32)).astype(jnp.bfloat16)
    pair_lags = jnp.einsum(
        "krij,rkl->ijl", high, table, preferred_element_type=jnp.float32
    ) + jnp.einsum("krij,rkl->ijl", low, table, preferred_element_type=jnp.float32)
    norm_scale = 1.0 / math.sqrt(freq_count * seg_count * time_count)
    return pair_lags * norm_scale


def solution(mesh):
    return jax.shard_map(
        per_device,
        mesh=mesh,
        in_specs=(P("tm", "chan", None),),
        out_specs=P(("chan", "tm"), None, None),
        check_vma=False,
    )
```

```python
import math

import jax
import jax.numpy as jnp
from jax import lax
from jax.sharding import PartitionSpec as P

LAGS = 256


def whiten(real_part, imag_part):
    power = real_part * real_part + imag_part * imag_part
    level = jnp.mean(power, axis=-1, keepdims=True)
    factor = 1.0 / jnp.sqrt(power + 0.1 * level + 1e-06)
    return (real_part * factor, imag_part * factor)


def lag_table(freq_count, sample_count, lag_count):
    freq_index = jnp.arange(1, freq_count + 1, dtype=jnp.int32)
    lag_index = jnp.arange(lag_count, dtype=jnp.int32) - lag_count // 2
    turns = freq_index[:, None] * (lag_index[None, :] % sample_count) % sample_count
    angle = turns.astype(jnp.float32) * (2.0 * math.pi / sample_count)
    return jnp.concatenate([jnp.cos(angle), -jnp.sin(angle)], axis=0).astype(jnp.bfloat16)


def transform_tables(sample_count, freq_count):
    time_index = jnp.arange(sample_count, dtype=jnp.int32)
    freq_index = jnp.arange(1, freq_count + 1, dtype=jnp.int32)
    turns = time_index[:, None] * freq_index[None, :] % sample_count
    angle = turns.astype(jnp.float32) * (2.0 * math.pi / sample_count)
    return (jnp.cos(angle), -jnp.sin(angle))


def per_device(raw_samples):
    seg_count, block_width, raw_length = raw_samples.shape
    sample_count = raw_length // 2
    freq_count = sample_count // 8
    chan_count = lax.axis_size("chan")
    time_count = lax.axis_size("tm")
    channel_total = block_width * chan_count
    row_width = channel_total // (chan_count * time_count)
    raw_rows = raw_samples.reshape(seg_count * block_width, raw_length)
    cos_table, sin_table = transform_tables(sample_count, freq_count)
    both_tables = jnp.concatenate([cos_table, sin_table], axis=1)
    next_tables = jnp.concatenate([both_tables[1:], jnp.zeros_like(both_tables[:1])], axis=0)
    folded = jnp.stack([0.5 * both_tables, 0.25 * both_tables + 0.25 * next_tables], axis=1)
    folded = folded.reshape(raw_length, 2 * freq_count)
    spectrum = jnp.dot(
        raw_rows, folded, precision=lax.Precision.HIGHEST, preferred_element_type=jnp.float32
    )
    real_part = spectrum[:, :freq_count].reshape(seg_count, block_width, freq_count)
    imag_part = spectrum[:, freq_count:].reshape(seg_count, block_width, freq_count)
    real_w, imag_w = whiten(real_part, imag_part)
    local_spec = jnp.stack([real_w, imag_w], axis=0).astype(jnp.bfloat16)
    every = lax.all_gather(local_spec, ("chan", "tm"), axis=0)
    every = every.reshape(chan_count, time_count, 2, seg_count, block_width, freq_count)
    chan_index = lax.axis_index("chan")
    tm_index = lax.axis_index("tm")
    own_block = lax.dynamic_index_in_dim(every, chan_index, 0, keepdims=False)
    rows = lax.dynamic_slice_in_dim(own_block, tm_index * row_width, row_width, axis=3)
    turned = jnp.stack([rows[:, 1], -rows[:, 0]], axis=1)
    left = jnp.concatenate([rows, turned], axis=3)
    cross = jnp.einsum("trsak,ctrswk->kacw", left, every, preferred_element_type=jnp.float32)
    cross = cross.reshape(freq_count, 2, row_width, channel_total)
    table = lag_table(freq_count, sample_count, LAGS).reshape(2, freq_count, LAGS)
    high = cross.astype(jnp.bfloat16)
    low = (cross - high.astype(jnp.float32)).astype(jnp.bfloat16)
    pair_lags = jnp.einsum(
        "krij,rkl->ijl", high, table, preferred_element_type=jnp.float32
    ) + jnp.einsum("krij,rkl->ijl", low, table, preferred_element_type=jnp.float32)
    norm_scale = 1.0 / math.sqrt(freq_count * seg_count * time_count)
    return pair_lags * norm_scale


def solution(mesh):
    return jax.shard_map(
        per_device,
        mesh=mesh,
        in_specs=(P("tm", "chan", None),),
        out_specs=P(("chan", "tm"), None, None),
        check_vma=False,
    )
```

```python
import math

import jax
import jax.numpy as jnp
from jax import lax
from jax.sharding import PartitionSpec as P

LAGS = 256


def whiten(real_part, imag_part):
    power = real_part * real_part + imag_part * imag_part
    level = jnp.mean(power, axis=-1, keepdims=True)
    factor = 1.0 / jnp.sqrt(power + 0.1 * level + 1e-06)
    return (real_part * factor, imag_part * factor)


def lag_table(freq_count, sample_count, lag_count):
    freq_index = jnp.arange(1, freq_count + 1, dtype=jnp.int32)
    lag_index = jnp.arange(lag_count, dtype=jnp.int32) - lag_count // 2
    turns = freq_index[:, None] * (lag_index[None, :] % sample_count) % sample_count
    angle = turns.astype(jnp.float32) * (2.0 * math.pi / sample_count)
    return jnp.concatenate([jnp.cos(angle), -jnp.sin(angle)], axis=0).astype(jnp.bfloat16)


def folded_tables(sample_count, freq_count):
    raw_index = jnp.arange(2 * sample_count, dtype=jnp.int32)[:, None]
    freq_index = jnp.arange(1, freq_count + 1, dtype=jnp.int32)[None, :]
    base_time = raw_index // 2
    odd = (raw_index % 2) == 1
    scale = 2.0 * math.pi / sample_count
    first_angle = (base_time * freq_index % sample_count).astype(jnp.float32) * scale
    second_angle = ((base_time + 1) * freq_index % sample_count).astype(jnp.float32) * scale
    has_next = odd & (base_time + 1 < sample_count)
    first_weight = jnp.where(odd, 0.25, 0.5)
    second_weight = jnp.where(has_next, 0.25, 0.0)
    cos_part = first_weight * jnp.cos(first_angle) + second_weight * jnp.cos(second_angle)
    sin_part = -(first_weight * jnp.sin(first_angle) + second_weight * jnp.sin(second_angle))
    return jnp.concatenate([cos_part, sin_part], axis=1)


def per_device(raw_samples):
    seg_count, block_width, raw_length = raw_samples.shape
    sample_count = raw_length // 2
    freq_count = sample_count // 8
    chan_count = lax.axis_size("chan")
    time_count = lax.axis_size("zz") * lax.axis_size("core")
    channel_total = block_width * chan_count
    row_width = channel_total // (chan_count * time_count)
    raw_rows = raw_samples.reshape(seg_count * block_width, raw_length)
    folded = folded_tables(sample_count, freq_count)
    spectrum = jnp.dot(
        raw_rows, folded, precision=lax.Precision.HIGH, preferred_element_type=jnp.float32
    )
    real_part = spectrum[:, :freq_count].reshape(seg_count, block_width, freq_count)
    imag_part = spectrum[:, freq_count:].reshape(seg_count, block_width, freq_count)
    real_w, imag_w = whiten(real_part, imag_part)
    local_spec = jnp.stack([real_w, imag_w], axis=0).astype(jnp.bfloat16)
    core_count = 2
    same_core = lax.all_gather(local_spec, ("chan", "zz"), axis=0)
    every = lax.all_gather(same_core, "core", axis=0)
    every = every.reshape(
        core_count, chan_count, time_count // core_count, 2, seg_count, block_width, freq_count
    )
    chan_index = lax.axis_index("chan")
    tm_index = lax.axis_index("zz") * core_count + lax.axis_index("core")
    own_block = lax.dynamic_index_in_dim(every, chan_index, 1, keepdims=False)
    rows = lax.dynamic_slice_in_dim(own_block, tm_index * row_width, row_width, axis=4)
    turned = jnp.stack([rows[:, :, 1], -rows[:, :, 0]], axis=2)
    left = jnp.concatenate([rows, turned], axis=4)
    cross = jnp.einsum("hzrsak,hczrswk->kacw", left, every, preferred_element_type=jnp.float32)
    cross = cross.reshape(freq_count, 2, row_width, channel_total)
    table = lag_table(freq_count, sample_count, LAGS).reshape(2, freq_count, LAGS)
    high = cross.astype(jnp.bfloat16)
    low = (cross - high.astype(jnp.float32)).astype(jnp.bfloat16)
    pair_lags = jnp.einsum(
        "krij,rkl->ijl", high, table, preferred_element_type=jnp.float32
    ) + jnp.einsum("krij,rkl->ijl", low, table, preferred_element_type=jnp.float32)
    norm_scale = 1.0 / math.sqrt(freq_count * seg_count * time_count)
    return pair_lags * norm_scale


def solution(mesh):
    chan_count, time_count = mesh.devices.shape
    split_mesh = jax.sharding.Mesh(
        mesh.devices.reshape(chan_count, time_count // 2, 2), ("chan", "zz", "core")
    )
    return jax.shard_map(
        per_device,
        mesh=split_mesh,
        in_specs=(P(("zz", "core"), "chan", None),),
        out_specs=P(("chan", "zz", "core"), None, None),
        check_vma=False,
    )
```

```python
import math

import jax
import jax.numpy as jnp
from jax import lax
from jax.sharding import PartitionSpec as P

LAGS = 256


def whiten(real_part, imag_part):
    power = real_part * real_part + imag_part * imag_part
    level = jnp.mean(power, axis=-1, keepdims=True)
    factor = 1.0 / jnp.sqrt(power + 0.1 * level + 1e-06)
    return (real_part * factor, imag_part * factor)


def lag_table(freq_count, sample_count, lag_count):
    freq_index = jnp.arange(1, freq_count + 1, dtype=jnp.int32)
    lag_index = jnp.arange(lag_count, dtype=jnp.int32) - lag_count // 2
    turns = freq_index[:, None] * (lag_index[None, :] % sample_count) % sample_count
    angle = turns.astype(jnp.float32) * (2.0 * math.pi / sample_count)
    return jnp.concatenate([jnp.cos(angle), -jnp.sin(angle)], axis=0).astype(jnp.bfloat16)


def folded_tables(sample_count, freq_count):
    fine_rows = 64
    coarse_rows = 2 * sample_count // fine_rows
    scale = 2.0 * math.pi / sample_count
    freq_index = jnp.arange(1, freq_count + 1, dtype=jnp.int32)[None, None, :]
    coarse_time = jnp.arange(coarse_rows, dtype=jnp.int32)[:, None, None] * (fine_rows // 2)
    fine = jnp.arange(fine_rows, dtype=jnp.int32)[None, :, None]
    fine_time = fine // 2
    odd = (fine % 2) == 1

    def angle(times):
        return (times * freq_index % sample_count).astype(jnp.float32) * scale

    coarse_angle = angle(coarse_time)
    coarse_cos, coarse_sin = jnp.cos(coarse_angle), jnp.sin(coarse_angle)
    this_angle = angle(fine_time)
    next_angle = angle(fine_time + 1)
    this_cos = coarse_cos * jnp.cos(this_angle) - coarse_sin * jnp.sin(this_angle)
    this_sin = coarse_sin * jnp.cos(this_angle) + coarse_cos * jnp.sin(this_angle)
    next_cos = coarse_cos * jnp.cos(next_angle) - coarse_sin * jnp.sin(next_angle)
    next_sin = coarse_sin * jnp.cos(next_angle) + coarse_cos * jnp.sin(next_angle)
    last_row = (coarse_time + fine_time + 1) >= sample_count
    this_weight = jnp.where(odd, 0.25, 0.5)
    next_weight = jnp.where(odd & ~last_row, 0.25, 0.0)
    cos_part = this_weight * this_cos + next_weight * next_cos
    sin_part = -(this_weight * this_sin + next_weight * next_sin)
    both = jnp.concatenate([cos_part, sin_part], axis=-1)
    return both.reshape(2 * sample_count, 2 * freq_count)


def per_device(raw_samples):
    seg_count, block_width, raw_length = raw_samples.shape
    sample_count = raw_length // 2
    freq_count = sample_count // 8
    chan_count = lax.axis_size("chan")
    time_count = lax.axis_size("tm")
    channel_total = block_width * chan_count
    row_width = channel_total // (chan_count * time_count)
    raw_rows = raw_samples.reshape(seg_count * block_width, raw_length)
    folded = folded_tables(sample_count, freq_count)
    spectrum = jnp.dot(
        raw_rows, folded, precision=lax.Precision.HIGH, preferred_element_type=jnp.float32
    )
    real_part = spectrum[:, :freq_count].reshape(seg_count, block_width, freq_count)
    imag_part = spectrum[:, freq_count:].reshape(seg_count, block_width, freq_count)
    real_w, imag_w = whiten(real_part, imag_part)
    local_spec = jnp.stack([real_w, imag_w], axis=0).astype(jnp.bfloat16)
    every = lax.all_gather(local_spec, ("chan", "tm"), axis=0)
    every = every.reshape(chan_count, time_count, 2, seg_count, block_width, freq_count)
    chan_index = lax.axis_index("chan")
    tm_index = lax.axis_index("tm")
    own_block = lax.dynamic_index_in_dim(every, chan_index, 0, keepdims=False)
    rows = lax.dynamic_slice_in_dim(own_block, tm_index * row_width, row_width, axis=3)
    turned = jnp.stack([rows[:, 1], -rows[:, 0]], axis=1)
    left = jnp.concatenate([rows, turned], axis=3)
    cross = jnp.einsum("trsak,ctrswk->kacw", left, every, preferred_element_type=jnp.float32)
    cross = cross.reshape(freq_count, 2, row_width, channel_total)
    table = lag_table(freq_count, sample_count, LAGS).reshape(2, freq_count, LAGS)
    high = cross.astype(jnp.bfloat16)
    low = (cross - high.astype(jnp.float32)).astype(jnp.bfloat16)
    pair_lags = jnp.einsum(
        "krij,rkl->ijl", high, table, preferred_element_type=jnp.float32
    ) + jnp.einsum("krij,rkl->ijl", low, table, preferred_element_type=jnp.float32)
    norm_scale = 1.0 / math.sqrt(freq_count * seg_count * time_count)
    return pair_lags * norm_scale


def solution(mesh):
    return jax.shard_map(
        per_device,
        mesh=mesh,
        in_specs=(P("tm", "chan", None),),
        out_specs=P(("chan", "tm"), None, None),
        check_vma=False,
    )
```

```python
import math

import jax
import jax.numpy as jnp
from jax import lax
from jax.sharding import PartitionSpec as P

LAGS = 256


def whiten(real_part, imag_part):
    power = real_part * real_part + imag_part * imag_part
    level = jnp.mean(power, axis=-1, keepdims=True)
    factor = 1.0 / jnp.sqrt(power + 0.1 * level + 1e-06)
    return (real_part * factor, imag_part * factor)


def lag_table(freq_count, sample_count, lag_count):
    freq_index = jnp.arange(1, freq_count + 1, dtype=jnp.int32)
    lag_index = jnp.arange(lag_count, dtype=jnp.int32) - lag_count // 2
    turns = freq_index[:, None] * (lag_index[None, :] % sample_count) % sample_count
    angle = turns.astype(jnp.float32) * (2.0 * math.pi / sample_count)
    return jnp.concatenate([jnp.cos(angle), -jnp.sin(angle)], axis=0).astype(jnp.bfloat16)


def folded_tables(sample_count, freq_count):
    fine_rows = 64
    coarse_rows = 2 * sample_count // fine_rows
    scale = 2.0 * math.pi / sample_count
    freq_index = jnp.arange(1, freq_count + 1, dtype=jnp.int32)[None, None, :]
    coarse_time = jnp.arange(coarse_rows, dtype=jnp.int32)[:, None, None] * (fine_rows // 2)
    fine = jnp.arange(fine_rows, dtype=jnp.int32)[None, :, None]
    fine_time = fine // 2
    odd = (fine % 2) == 1

    def angle(times):
        return (times * freq_index % sample_count).astype(jnp.float32) * scale

    coarse_angle = angle(coarse_time)
    coarse_cos, coarse_sin = jnp.cos(coarse_angle), jnp.sin(coarse_angle)
    this_angle = angle(fine_time)
    next_angle = angle(fine_time + 1)
    this_cos = coarse_cos * jnp.cos(this_angle) - coarse_sin * jnp.sin(this_angle)
    this_sin = coarse_sin * jnp.cos(this_angle) + coarse_cos * jnp.sin(this_angle)
    next_cos = coarse_cos * jnp.cos(next_angle) - coarse_sin * jnp.sin(next_angle)
    next_sin = coarse_sin * jnp.cos(next_angle) + coarse_cos * jnp.sin(next_angle)
    last_row = (coarse_time + fine_time + 1) >= sample_count
    this_weight = jnp.where(odd, 0.25, 0.5)
    next_weight = jnp.where(odd & ~last_row, 0.25, 0.0)
    cos_part = this_weight * this_cos + next_weight * next_cos
    sin_part = -(this_weight * this_sin + next_weight * next_sin)
    both = jnp.concatenate([cos_part, sin_part], axis=-1)
    return both.reshape(2 * sample_count, 2 * freq_count)


def per_device(raw_samples):
    seg_count, block_width, raw_length = raw_samples.shape
    sample_count = raw_length // 2
    freq_count = sample_count // 8
    chan_count = lax.axis_size("chan")
    time_count = lax.axis_size("tm")
    channel_total = block_width * chan_count
    row_width = channel_total // (chan_count * time_count)
    raw_rows = raw_samples.reshape(seg_count * block_width, raw_length)
    folded = folded_tables(sample_count, freq_count)
    spectrum = jnp.dot(
        raw_rows, folded, precision=lax.Precision.HIGH, preferred_element_type=jnp.float32
    )
    real_part = spectrum[:, :freq_count].reshape(seg_count, block_width, freq_count)
    imag_part = spectrum[:, freq_count:].reshape(seg_count, block_width, freq_count)
    real_w, imag_w = whiten(real_part, imag_part)
    local_spec = jnp.stack([real_w, imag_w], axis=0).astype(jnp.bfloat16)
    local_spec = jnp.transpose(local_spec, (3, 0, 1, 2)).reshape(
        freq_count, 2 * seg_count, block_width
    )
    every = lax.all_gather(local_spec, ("chan", "tm"), axis=1)
    every = every.reshape(freq_count, chan_count, time_count, 2 * seg_count, block_width)
    chan_index = lax.axis_index("chan")
    tm_index = lax.axis_index("tm")
    own_block = lax.dynamic_index_in_dim(every, chan_index, 1, keepdims=False)
    rows = lax.dynamic_slice_in_dim(own_block, tm_index * row_width, row_width, axis=3)
    rows = rows.reshape(freq_count, time_count, 2, seg_count, row_width)
    turned = jnp.stack([rows[:, :, 1], -rows[:, :, 0]], axis=2)
    left = jnp.concatenate([rows, turned], axis=4).reshape(
        freq_count, time_count * 2 * seg_count, 2 * row_width
    )
    every = every.reshape(freq_count, chan_count, time_count * 2 * seg_count, block_width)
    table = lag_table(freq_count, sample_count, LAGS).reshape(2, freq_count, LAGS)
    column_blocks = []
    for column_chan in range(chan_count):
        cross = jnp.einsum(
            "kqa,kqw->kaw", left, every[:, column_chan], preferred_element_type=jnp.float32
        )
        cross = cross.reshape(freq_count, 2, row_width, block_width)
        high = cross.astype(jnp.bfloat16)
        low = (cross - high.astype(jnp.float32)).astype(jnp.bfloat16)
        column_blocks.append(
            jnp.einsum("kriw,rkl->iwl", high, table, preferred_element_type=jnp.float32)
            + jnp.einsum("kriw,rkl->iwl", low, table, preferred_element_type=jnp.float32)
        )
    pair_lags = jnp.concatenate(column_blocks, axis=1)
    norm_scale = 1.0 / math.sqrt(freq_count * seg_count * time_count)
    return pair_lags * norm_scale


def solution(mesh):
    return jax.shard_map(
        per_device,
        mesh=mesh,
        in_specs=(P("tm", "chan", None),),
        out_specs=P(("chan", "tm"), None, None),
        check_vma=False,
    )
```

```python
import math

import jax
import jax.numpy as jnp
from jax import lax
from jax.sharding import PartitionSpec as P

LAGS = 256


def whiten(real_part, imag_part):
    power = real_part * real_part + imag_part * imag_part
    level = jnp.mean(power, axis=-1, keepdims=True)
    factor = 1.0 / jnp.sqrt(power + 0.1 * level + 1e-06)
    return (real_part * factor, imag_part * factor)


def lag_table(freq_count, sample_count, lag_count):
    freq_index = jnp.arange(1, freq_count + 1, dtype=jnp.int32)
    lag_index = jnp.arange(lag_count, dtype=jnp.int32) - lag_count // 2
    turns = freq_index[:, None] * (lag_index[None, :] % sample_count) % sample_count
    angle = turns.astype(jnp.float32) * (2.0 * math.pi / sample_count)
    return jnp.concatenate([jnp.cos(angle), -jnp.sin(angle)], axis=0).astype(jnp.bfloat16)


def folded_tables(sample_count, freq_count):
    fine_rows = 64
    coarse_rows = 2 * sample_count // fine_rows
    scale = 2.0 * math.pi / sample_count
    freq_index = jnp.arange(1, freq_count + 1, dtype=jnp.int32)[None, None, :]
    coarse_time = jnp.arange(coarse_rows, dtype=jnp.int32)[:, None, None] * (fine_rows // 2)
    fine = jnp.arange(fine_rows, dtype=jnp.int32)[None, :, None]
    fine_time = fine // 2
    odd = (fine % 2) == 1

    def angle(times):
        return (times * freq_index % sample_count).astype(jnp.float32) * scale

    coarse_angle = angle(coarse_time)
    coarse_cos, coarse_sin = jnp.cos(coarse_angle), jnp.sin(coarse_angle)
    this_angle = angle(fine_time)
    next_angle = angle(fine_time + 1)
    this_cos = coarse_cos * jnp.cos(this_angle) - coarse_sin * jnp.sin(this_angle)
    this_sin = coarse_sin * jnp.cos(this_angle) + coarse_cos * jnp.sin(this_angle)
    next_cos = coarse_cos * jnp.cos(next_angle) - coarse_sin * jnp.sin(next_angle)
    next_sin = coarse_sin * jnp.cos(next_angle) + coarse_cos * jnp.sin(next_angle)
    last_row = (coarse_time + fine_time + 1) >= sample_count
    this_weight = jnp.where(odd, 0.25, 0.5)
    next_weight = jnp.where(odd & ~last_row, 0.25, 0.0)
    cos_part = this_weight * this_cos + next_weight * next_cos
    sin_part = -(this_weight * this_sin + next_weight * next_sin)
    both = jnp.concatenate([cos_part, sin_part], axis=-1)
    return both.reshape(2 * sample_count, 2 * freq_count)


def per_device(raw_samples):
    seg_count, block_width, raw_length = raw_samples.shape
    sample_count = raw_length // 2
    freq_count = sample_count // 8
    chan_count = lax.axis_size("chan")
    time_count = lax.axis_size("tm")
    channel_total = block_width * chan_count
    row_width = channel_total // (chan_count * time_count)
    raw_rows = raw_samples.reshape(seg_count * block_width, raw_length)
    folded = folded_tables(sample_count, freq_count)
    spectrum = jnp.dot(
        raw_rows, folded, precision=lax.Precision.HIGH, preferred_element_type=jnp.float32
    )
    real_part = spectrum[:, :freq_count].reshape(seg_count, block_width, freq_count)
    imag_part = spectrum[:, freq_count:].reshape(seg_count, block_width, freq_count)
    real_w, imag_w = whiten(real_part, imag_part)
    local_spec = jnp.stack([real_w, imag_w], axis=0).astype(jnp.bfloat16)
    every = lax.all_gather(local_spec, ("chan", "tm"), axis=0)
    every = every.reshape(chan_count, time_count, 2, seg_count, block_width, freq_count)
    chan_index = lax.axis_index("chan")
    tm_index = lax.axis_index("tm")
    own_block = lax.dynamic_index_in_dim(every, chan_index, 0, keepdims=False)
    rows = lax.dynamic_slice_in_dim(own_block, tm_index * row_width, row_width, axis=3)
    turned = jnp.stack([rows[:, 1], -rows[:, 0]], axis=1)
    left = jnp.concatenate([rows, turned], axis=3)
    cross = jnp.einsum("trsak,ctrswk->kacw", left, every, preferred_element_type=jnp.bfloat16)
    cross = cross.reshape(freq_count, 2, row_width, channel_total)
    table = lag_table(freq_count, sample_count, LAGS).reshape(2, freq_count, LAGS)
    pair_lags = jnp.einsum("krij,rkl->ijl", cross, table, preferred_element_type=jnp.float32)
    norm_scale = 1.0 / math.sqrt(freq_count * seg_count * time_count)
    return pair_lags * norm_scale


def solution(mesh):
    return jax.shard_map(
        per_device,
        mesh=mesh,
        in_specs=(P("tm", "chan", None),),
        out_specs=P(("chan", "tm"), None, None),
        check_vma=False,
    )
```

```python
import math

import jax
import jax.numpy as jnp
from jax import lax
from jax.sharding import PartitionSpec as P

LAGS = 256


def whiten(real_part, imag_part):
    power = real_part * real_part + imag_part * imag_part
    level = jnp.mean(power, axis=-1, keepdims=True)
    factor = 1.0 / jnp.sqrt(power + 0.1 * level + 1e-06)
    return (real_part * factor, imag_part * factor)


def lag_table(freq_count, sample_count, lag_count):
    freq_index = jnp.arange(1, freq_count + 1, dtype=jnp.int32)
    lag_index = jnp.arange(lag_count, dtype=jnp.int32) - lag_count // 2
    turns = freq_index[:, None] * (lag_index[None, :] % sample_count) % sample_count
    angle = turns.astype(jnp.float32) * (2.0 * math.pi / sample_count)
    return jnp.concatenate([jnp.cos(angle), -jnp.sin(angle)], axis=0).astype(jnp.bfloat16)


def folded_tables(sample_count, freq_count):
    fine_rows = 64
    coarse_rows = 2 * sample_count // fine_rows
    scale = 2.0 * math.pi / sample_count
    freq_index = jnp.arange(1, freq_count + 1, dtype=jnp.int32)[None, None, :]
    coarse_time = jnp.arange(coarse_rows, dtype=jnp.int32)[:, None, None] * (fine_rows // 2)
    fine = jnp.arange(fine_rows, dtype=jnp.int32)[None, :, None]
    fine_time = fine // 2
    odd = (fine % 2) == 1

    def angle(times):
        return (times * freq_index % sample_count).astype(jnp.float32) * scale

    coarse_angle = angle(coarse_time)
    coarse_cos, coarse_sin = jnp.cos(coarse_angle), jnp.sin(coarse_angle)
    this_angle = angle(fine_time)
    next_angle = angle(fine_time + 1)
    this_cos = coarse_cos * jnp.cos(this_angle) - coarse_sin * jnp.sin(this_angle)
    this_sin = coarse_sin * jnp.cos(this_angle) + coarse_cos * jnp.sin(this_angle)
    next_cos = coarse_cos * jnp.cos(next_angle) - coarse_sin * jnp.sin(next_angle)
    next_sin = coarse_sin * jnp.cos(next_angle) + coarse_cos * jnp.sin(next_angle)
    last_row = (coarse_time + fine_time + 1) >= sample_count
    this_weight = jnp.where(odd, 0.25, 0.5)
    next_weight = jnp.where(odd & ~last_row, 0.25, 0.0)
    cos_part = this_weight * this_cos + next_weight * next_cos
    sin_part = -(this_weight * this_sin + next_weight * next_sin)
    both = jnp.concatenate([cos_part, sin_part], axis=-1)
    return both.reshape(2 * sample_count, 2 * freq_count)


def per_device(raw_samples):
    seg_count, block_width, raw_length = raw_samples.shape
    sample_count = raw_length // 2
    freq_count = sample_count // 8
    chan_count = lax.axis_size("chan")
    time_count = lax.axis_size("tm")
    channel_total = block_width * chan_count
    row_width = channel_total // (chan_count * time_count)
    raw_rows = raw_samples.reshape(seg_count * block_width, raw_length)
    folded = folded_tables(sample_count, freq_count)
    spectrum = jnp.dot(
        raw_rows, folded, precision=lax.Precision.HIGH, preferred_element_type=jnp.float32
    )
    real_part = spectrum[:, :freq_count].reshape(seg_count, block_width, freq_count)
    imag_part = spectrum[:, freq_count:].reshape(seg_count, block_width, freq_count)
    real_w, imag_w = whiten(real_part, imag_part)
    local_spec = jnp.stack([real_w, imag_w], axis=0).astype(jnp.bfloat16)
    local_spec = jnp.transpose(local_spec, (3, 0, 1, 2))
    every = lax.all_gather(local_spec, ("chan", "tm"), axis=0)
    every = every.reshape(chan_count, time_count, freq_count, 2, seg_count, block_width)
    chan_index = lax.axis_index("chan")
    tm_index = lax.axis_index("tm")
    own_block = lax.dynamic_index_in_dim(every, chan_index, 0, keepdims=False)
    row_ids = tm_index * row_width + jnp.arange(row_width, dtype=jnp.int32)
    pick = (jnp.arange(block_width, dtype=jnp.int32)[:, None] == row_ids[None, :])
    rows = jnp.einsum(
        "tkrsw,wi->tkrsi", own_block, pick.astype(jnp.bfloat16),
        preferred_element_type=jnp.float32,
    ).astype(jnp.bfloat16)
    turned = jnp.stack([rows[:, :, 1], -rows[:, :, 0]], axis=2)
    left = jnp.concatenate([rows, turned], axis=4)
    cross = jnp.einsum("tkrsa,ctkrsw->kacw", left, every, preferred_element_type=jnp.bfloat16)
    cross = cross.reshape(freq_count, 2, row_width, channel_total)
    table = lag_table(freq_count, sample_count, LAGS).reshape(2, freq_count, LAGS)
    pair_lags = jnp.einsum("krij,rkl->ijl", cross, table, preferred_element_type=jnp.float32)
    norm_scale = 1.0 / math.sqrt(freq_count * seg_count * time_count)
    return pair_lags * norm_scale


def solution(mesh):
    return jax.shard_map(
        per_device,
        mesh=mesh,
        in_specs=(P("tm", "chan", None),),
        out_specs=P(("chan", "tm"), None, None),
        check_vma=False,
    )
```

```python
import math

import jax
import jax.numpy as jnp
from jax import lax
from jax.sharding import PartitionSpec as P

LAGS = 256


def whiten(real_part, imag_part):
    power = real_part * real_part + imag_part * imag_part
    level = jnp.mean(power, axis=-1, keepdims=True)
    factor = 1.0 / jnp.sqrt(power + 0.1 * level + 1e-06)
    return (real_part * factor, imag_part * factor)


def lag_table(freq_count, sample_count, lag_count):
    freq_index = jnp.arange(1, freq_count + 1, dtype=jnp.int32)
    lag_index = jnp.arange(lag_count, dtype=jnp.int32) - lag_count // 2
    turns = freq_index[:, None] * (lag_index[None, :] % sample_count) % sample_count
    angle = turns.astype(jnp.float32) * (2.0 * math.pi / sample_count)
    return jnp.concatenate([jnp.cos(angle), -jnp.sin(angle)], axis=0).astype(jnp.bfloat16)


def folded_tables(sample_count, freq_count):
    fine_rows = 64
    coarse_rows = 2 * sample_count // fine_rows
    scale = 2.0 * math.pi / sample_count
    freq_index = jnp.arange(1, freq_count + 1, dtype=jnp.int32)[None, None, :]
    coarse_time = jnp.arange(coarse_rows, dtype=jnp.int32)[:, None, None] * (fine_rows // 2)
    fine = jnp.arange(fine_rows, dtype=jnp.int32)[None, :, None]
    fine_time = fine // 2
    odd = (fine % 2) == 1

    def angle(times):
        return (times * freq_index % sample_count).astype(jnp.float32) * scale

    coarse_angle = angle(coarse_time)
    coarse_cos, coarse_sin = jnp.cos(coarse_angle), jnp.sin(coarse_angle)
    this_angle = angle(fine_time)
    next_angle = angle(fine_time + 1)
    this_cos = coarse_cos * jnp.cos(this_angle) - coarse_sin * jnp.sin(this_angle)
    this_sin = coarse_sin * jnp.cos(this_angle) + coarse_cos * jnp.sin(this_angle)
    next_cos = coarse_cos * jnp.cos(next_angle) - coarse_sin * jnp.sin(next_angle)
    next_sin = coarse_sin * jnp.cos(next_angle) + coarse_cos * jnp.sin(next_angle)
    last_row = (coarse_time + fine_time + 1) >= sample_count
    this_weight = jnp.where(odd, 0.25, 0.5)
    next_weight = jnp.where(odd & ~last_row, 0.25, 0.0)
    cos_part = this_weight * this_cos + next_weight * next_cos
    sin_part = -(this_weight * this_sin + next_weight * next_sin)
    both = jnp.concatenate([cos_part, sin_part], axis=-1)
    return both.reshape(2 * sample_count, 2 * freq_count)


def per_device(raw_samples):
    seg_count, block_width, raw_length = raw_samples.shape
    sample_count = raw_length // 2
    freq_count = sample_count // 8
    chan_count = lax.axis_size("chan")
    time_count = lax.axis_size("tm")
    channel_total = block_width * chan_count
    row_width = channel_total // (chan_count * time_count)
    raw_rows = raw_samples.reshape(seg_count * block_width, raw_length)
    folded = folded_tables(sample_count, freq_count)
    spectrum = jnp.dot(
        raw_rows, folded, precision=lax.Precision.HIGH, preferred_element_type=jnp.float32
    )
    real_part = spectrum[:, :freq_count].reshape(seg_count, block_width, freq_count)
    imag_part = spectrum[:, freq_count:].reshape(seg_count, block_width, freq_count)
    real_w, imag_w = whiten(real_part, imag_part)
    local_spec = jnp.stack([real_w, imag_w], axis=0).astype(jnp.bfloat16)
    local_spec = jnp.transpose(local_spec, (3, 0, 1, 2)).reshape(
        freq_count, 2 * seg_count, block_width
    )
    every = lax.all_gather(local_spec, ("chan", "tm"), axis=0)
    every = every.reshape(chan_count, time_count, freq_count, 2 * seg_count, block_width)
    chan_index = lax.axis_index("chan")
    tm_index = lax.axis_index("tm")
    own_block = lax.dynamic_index_in_dim(every, chan_index, 0, keepdims=False)
    row_ids = tm_index * row_width + jnp.arange(row_width, dtype=jnp.int32)
    pick = (jnp.arange(block_width, dtype=jnp.int32)[:, None] == row_ids[None, :])
    rows = jnp.einsum(
        "tkqw,wi->tkqi", own_block, pick.astype(jnp.bfloat16),
        preferred_element_type=jnp.float32,
    ).astype(jnp.bfloat16)
    rows = rows.reshape(time_count, freq_count, 2, seg_count, row_width)
    turned = jnp.stack([rows[:, :, 1], -rows[:, :, 0]], axis=2)
    left = jnp.concatenate([rows, turned], axis=4).reshape(
        time_count, freq_count, 2 * seg_count, 2 * row_width
    )
    cross = jnp.einsum("tkqa,ctkqw->kacw", left, every, preferred_element_type=jnp.bfloat16)
    cross = cross.reshape(freq_count, 2, row_width, channel_total)
    table = lag_table(freq_count, sample_count, LAGS).reshape(2, freq_count, LAGS)
    pair_lags = jnp.einsum("krij,rkl->ijl", cross, table, preferred_element_type=jnp.float32)
    norm_scale = 1.0 / math.sqrt(freq_count * seg_count * time_count)
    return pair_lags * norm_scale


def solution(mesh):
    return jax.shard_map(
        per_device,
        mesh=mesh,
        in_specs=(P("tm", "chan", None),),
        out_specs=P(("chan", "tm"), None, None),
        check_vma=False,
    )
```

```python
import math

import jax
import jax.numpy as jnp
from jax import lax
from jax.sharding import PartitionSpec as P

LAGS = 256


def whiten(real_part, imag_part):
    power = real_part * real_part + imag_part * imag_part
    level = jnp.mean(power, axis=-1, keepdims=True)
    factor = 1.0 / jnp.sqrt(power + 0.1 * level + 1e-06)
    return (real_part * factor, imag_part * factor)


def lag_table(freq_count, sample_count, lag_count):
    freq_index = jnp.arange(1, freq_count + 1, dtype=jnp.int32)
    lag_index = jnp.arange(lag_count, dtype=jnp.int32) - lag_count // 2
    turns = freq_index[:, None] * (lag_index[None, :] % sample_count) % sample_count
    angle = turns.astype(jnp.float32) * (2.0 * math.pi / sample_count)
    return jnp.concatenate([jnp.cos(angle), -jnp.sin(angle)], axis=0).astype(jnp.bfloat16)


def folded_tables(sample_count, freq_count):
    fine_rows = 64
    coarse_rows = 2 * sample_count // fine_rows
    scale = 2.0 * math.pi / sample_count
    freq_index = jnp.arange(1, freq_count + 1, dtype=jnp.int32)[None, None, :]
    coarse_time = jnp.arange(coarse_rows, dtype=jnp.int32)[:, None, None] * (fine_rows // 2)
    fine = jnp.arange(fine_rows, dtype=jnp.int32)[None, :, None]
    fine_time = fine // 2
    odd = (fine % 2) == 1

    def angle(times):
        return (times * freq_index % sample_count).astype(jnp.float32) * scale

    coarse_angle = angle(coarse_time)
    coarse_cos, coarse_sin = jnp.cos(coarse_angle), jnp.sin(coarse_angle)
    this_angle = angle(fine_time)
    next_angle = angle(fine_time + 1)
    this_cos = coarse_cos * jnp.cos(this_angle) - coarse_sin * jnp.sin(this_angle)
    this_sin = coarse_sin * jnp.cos(this_angle) + coarse_cos * jnp.sin(this_angle)
    next_cos = coarse_cos * jnp.cos(next_angle) - coarse_sin * jnp.sin(next_angle)
    next_sin = coarse_sin * jnp.cos(next_angle) + coarse_cos * jnp.sin(next_angle)
    last_row = (coarse_time + fine_time + 1) >= sample_count
    this_weight = jnp.where(odd, 0.25, 0.5)
    next_weight = jnp.where(odd & ~last_row, 0.25, 0.0)
    cos_part = this_weight * this_cos + next_weight * next_cos
    sin_part = -(this_weight * this_sin + next_weight * next_sin)
    both = jnp.concatenate([cos_part, sin_part], axis=-1)
    return both.reshape(2 * sample_count, 2 * freq_count)


def per_device(raw_samples):
    seg_count, block_width, raw_length = raw_samples.shape
    sample_count = raw_length // 2
    freq_count = sample_count // 8
    chan_count = lax.axis_size("chan")
    time_count = lax.axis_size("tm")
    channel_total = block_width * chan_count
    row_width = channel_total // (chan_count * time_count)
    raw_rows = raw_samples.reshape(seg_count * block_width, raw_length)
    folded = folded_tables(sample_count, freq_count)
    spectrum = jnp.dot(
        raw_rows, folded, precision=lax.Precision.HIGH, preferred_element_type=jnp.float32
    )
    real_part = spectrum[:, :freq_count].reshape(seg_count, block_width, freq_count)
    imag_part = spectrum[:, freq_count:].reshape(seg_count, block_width, freq_count)
    real_w, imag_w = whiten(real_part, imag_part)
    local_spec = jnp.stack([real_w, imag_w], axis=0).astype(jnp.bfloat16)
    local_spec = jnp.transpose(local_spec, (3, 0, 1, 2)).reshape(
        freq_count, 2 * seg_count, block_width
    )
    every = lax.all_gather(local_spec, ("chan", "tm"), axis=0)
    every = every.reshape(chan_count, time_count, freq_count, 2 * seg_count, block_width)
    chan_index = lax.axis_index("chan")
    tm_index = lax.axis_index("tm")
    own_block = lax.dynamic_index_in_dim(every, chan_index, 0, keepdims=False)
    row_ids = tm_index * row_width + jnp.arange(row_width, dtype=jnp.int32)
    pick = (jnp.arange(block_width, dtype=jnp.int32)[:, None] == row_ids[None, :])
    rows = jnp.einsum(
        "tkqw,wi->tkqi", own_block, pick.astype(jnp.bfloat16),
        preferred_element_type=jnp.float32,
    ).astype(jnp.bfloat16)
    rows = rows.reshape(time_count, freq_count, 2, seg_count, row_width)
    turned = jnp.stack([rows[:, :, 1], -rows[:, :, 0]], axis=2)
    left = jnp.concatenate([rows, turned], axis=4).reshape(
        time_count, freq_count, 2 * seg_count, 2 * row_width
    )
    norm_scale = 1.0 / math.sqrt(freq_count * seg_count * time_count)
    cross = jnp.einsum("tkqa,ctkqw->kacw", left, every, preferred_element_type=jnp.float32)
    cross = (cross * norm_scale).astype(jnp.bfloat16)
    cross = cross.reshape(freq_count, 2, row_width, channel_total)
    table = lag_table(freq_count, sample_count, LAGS).reshape(2, freq_count, LAGS)
    return jnp.einsum("krij,rkl->ijl", cross, table, preferred_element_type=jnp.float32)


def solution(mesh):
    return jax.shard_map(
        per_device,
        mesh=mesh,
        in_specs=(P("tm", "chan", None),),
        out_specs=P(("chan", "tm"), None, None),
        check_vma=False,
    )
```

```python
import math

import jax
import jax.numpy as jnp
from jax import lax
from jax.experimental import pallas as pl
from jax.sharding import PartitionSpec as P

LAGS = 256


def whiten(real_part, imag_part):
    power = real_part * real_part + imag_part * imag_part
    level = jnp.mean(power, axis=-1, keepdims=True)
    factor = 1.0 / jnp.sqrt(power + 0.1 * level + 1e-06)
    return (real_part * factor, imag_part * factor)


def lag_table(freq_count, sample_count, lag_count):
    freq_index = jnp.arange(1, freq_count + 1, dtype=jnp.int32)
    lag_index = jnp.arange(lag_count, dtype=jnp.int32) - lag_count // 2
    turns = freq_index[:, None] * (lag_index[None, :] % sample_count) % sample_count
    angle = turns.astype(jnp.float32) * (2.0 * math.pi / sample_count)
    return jnp.concatenate([jnp.cos(angle), -jnp.sin(angle)], axis=0).astype(jnp.bfloat16)


def folded_tables(sample_count, freq_count):
    fine_rows = 64
    coarse_rows = 2 * sample_count // fine_rows
    scale = 2.0 * math.pi / sample_count
    freq_index = jnp.arange(1, freq_count + 1, dtype=jnp.int32)[None, None, :]
    coarse_time = jnp.arange(coarse_rows, dtype=jnp.int32)[:, None, None] * (fine_rows // 2)
    fine = jnp.arange(fine_rows, dtype=jnp.int32)[None, :, None]
    fine_time = fine // 2
    odd = (fine % 2) == 1

    def angle(times):
        return (times * freq_index % sample_count).astype(jnp.float32) * scale

    coarse_angle = angle(coarse_time)
    coarse_cos, coarse_sin = jnp.cos(coarse_angle), jnp.sin(coarse_angle)
    this_angle = angle(fine_time)
    next_angle = angle(fine_time + 1)
    this_cos = coarse_cos * jnp.cos(this_angle) - coarse_sin * jnp.sin(this_angle)
    this_sin = coarse_sin * jnp.cos(this_angle) + coarse_cos * jnp.sin(this_angle)
    next_cos = coarse_cos * jnp.cos(next_angle) - coarse_sin * jnp.sin(next_angle)
    next_sin = coarse_sin * jnp.cos(next_angle) + coarse_cos * jnp.sin(next_angle)
    last_row = (coarse_time + fine_time + 1) >= sample_count
    this_weight = jnp.where(odd, 0.25, 0.5)
    next_weight = jnp.where(odd & ~last_row, 0.25, 0.0)
    cos_part = this_weight * this_cos + next_weight * next_cos
    sin_part = -(this_weight * this_sin + next_weight * next_sin)
    both = jnp.concatenate([cos_part, sin_part], axis=-1)
    return both.reshape(2 * sample_count, 2 * freq_count)


def lag_kernel(cross_ref, table_ref, out_ref):
    row_width = out_ref.shape[0]
    table = table_ref[...]
    for row in range(row_width):
        real_rows = cross_ref[:, row, :].astype(jnp.float32)
        imag_rows = cross_ref[:, row_width + row, :].astype(jnp.float32)
        both = jnp.concatenate([real_rows, imag_rows], axis=0)
        out_ref[row] = jnp.dot(
            both.T.astype(jnp.bfloat16), table, preferred_element_type=jnp.float32
        )


def lag_transform(cross, table, interpret=False):
    freq_count, chan_count, pair_rows, block_width = cross.shape
    row_width = pair_rows // 2
    lag_count = table.shape[1]
    return pl.pallas_call(
        lag_kernel,
        grid=(chan_count,),
        in_specs=[
            pl.BlockSpec((freq_count, None, pair_rows, block_width), lambda c: (0, c, 0, 0)),
            pl.BlockSpec((2 * freq_count, lag_count), lambda c: (0, 0)),
        ],
        out_specs=pl.BlockSpec((row_width, block_width, lag_count), lambda c: (0, c, 0)),
        out_shape=jax.ShapeDtypeStruct((row_width, chan_count * block_width, lag_count), jnp.float32),
        interpret=interpret,
    )(cross, table)


def per_device(raw_samples):
    seg_count, block_width, raw_length = raw_samples.shape
    sample_count = raw_length // 2
    freq_count = sample_count // 8
    chan_count = lax.axis_size("chan")
    time_count = lax.axis_size("tm")
    channel_total = block_width * chan_count
    row_width = channel_total // (chan_count * time_count)
    raw_rows = raw_samples.reshape(seg_count * block_width, raw_length)
    folded = folded_tables(sample_count, freq_count)
    spectrum = jnp.dot(
        raw_rows, folded, precision=lax.Precision.HIGH, preferred_element_type=jnp.float32
    )
    real_part = spectrum[:, :freq_count].reshape(seg_count, block_width, freq_count)
    imag_part = spectrum[:, freq_count:].reshape(seg_count, block_width, freq_count)
    real_w, imag_w = whiten(real_part, imag_part)
    local_spec = jnp.stack([real_w, imag_w], axis=0).astype(jnp.bfloat16)
    local_spec = jnp.transpose(local_spec, (3, 0, 1, 2)).reshape(
        freq_count, 2 * seg_count, block_width
    )
    every = lax.all_gather(local_spec, ("chan", "tm"), axis=0)
    every = every.reshape(chan_count, time_count, freq_count, 2 * seg_count, block_width)
    chan_index = lax.axis_index("chan")
    tm_index = lax.axis_index("tm")
    own_block = lax.dynamic_index_in_dim(every, chan_index, 0, keepdims=False)
    row_ids = tm_index * row_width + jnp.arange(row_width, dtype=jnp.int32)
    pick = (jnp.arange(block_width, dtype=jnp.int32)[:, None] == row_ids[None, :])
    rows = jnp.einsum(
        "tkqw,wi->tkqi", own_block, pick.astype(jnp.bfloat16),
        preferred_element_type=jnp.float32,
    ).astype(jnp.bfloat16)
    rows = rows.reshape(time_count, freq_count, 2, seg_count, row_width)
    turned = jnp.stack([rows[:, :, 1], -rows[:, :, 0]], axis=2)
    left = jnp.concatenate([rows, turned], axis=4).reshape(
        time_count, freq_count, 2 * seg_count, 2 * row_width
    )
    norm_scale = 1.0 / math.sqrt(freq_count * seg_count * time_count)
    cross = jnp.einsum("tkqa,ctkqw->kcaw", left, every, preferred_element_type=jnp.float32)
    cross = (cross * norm_scale).astype(jnp.bfloat16)
    table = lag_table(freq_count, sample_count, LAGS)
    return lag_transform(cross, table)


def solution(mesh):
    return jax.shard_map(
        per_device,
        mesh=mesh,
        in_specs=(P("tm", "chan", None),),
        out_specs=P(("chan", "tm"), None, None),
        check_vma=False,
    )
```

```python
import math

import jax
import jax.numpy as jnp
from jax import lax
from jax.experimental import pallas as pl
from jax.sharding import PartitionSpec as P

LAGS = 256


def whiten(real_part, imag_part):
    power = real_part * real_part + imag_part * imag_part
    level = jnp.mean(power, axis=-1, keepdims=True)
    factor = 1.0 / jnp.sqrt(power + 0.1 * level + 1e-06)
    return (real_part * factor, imag_part * factor)


def lag_table(freq_count, sample_count, lag_count):
    freq_index = jnp.arange(1, freq_count + 1, dtype=jnp.int32)
    lag_index = jnp.arange(lag_count, dtype=jnp.int32) - lag_count // 2
    turns = freq_index[:, None] * (lag_index[None, :] % sample_count) % sample_count
    angle = turns.astype(jnp.float32) * (2.0 * math.pi / sample_count)
    return jnp.concatenate([jnp.cos(angle), -jnp.sin(angle)], axis=0).astype(jnp.bfloat16)


def folded_tables(sample_count, freq_count):
    fine_rows = 64
    coarse_rows = 2 * sample_count // fine_rows
    scale = 2.0 * math.pi / sample_count
    freq_index = jnp.arange(1, freq_count + 1, dtype=jnp.int32)[None, None, :]
    coarse_time = jnp.arange(coarse_rows, dtype=jnp.int32)[:, None, None] * (fine_rows // 2)
    fine = jnp.arange(fine_rows, dtype=jnp.int32)[None, :, None]
    fine_time = fine // 2
    odd = (fine % 2) == 1

    def angle(times):
        return (times * freq_index % sample_count).astype(jnp.float32) * scale

    coarse_angle = angle(coarse_time)
    coarse_cos, coarse_sin = jnp.cos(coarse_angle), jnp.sin(coarse_angle)
    this_angle = angle(fine_time)
    next_angle = angle(fine_time + 1)
    this_cos = coarse_cos * jnp.cos(this_angle) - coarse_sin * jnp.sin(this_angle)
    this_sin = coarse_sin * jnp.cos(this_angle) + coarse_cos * jnp.sin(this_angle)
    next_cos = coarse_cos * jnp.cos(next_angle) - coarse_sin * jnp.sin(next_angle)
    next_sin = coarse_sin * jnp.cos(next_angle) + coarse_cos * jnp.sin(next_angle)
    last_row = (coarse_time + fine_time + 1) >= sample_count
    this_weight = jnp.where(odd, 0.25, 0.5)
    next_weight = jnp.where(odd & ~last_row, 0.25, 0.0)
    cos_part = this_weight * this_cos + next_weight * next_cos
    sin_part = -(this_weight * this_sin + next_weight * next_sin)
    both = jnp.concatenate([cos_part, sin_part], axis=-1)
    return both.reshape(2 * sample_count, 2 * freq_count)


def lag_kernel(cross_ref, table_ref, out_ref):
    table = table_ref[...]
    for row in range(out_ref.shape[0]):
        real_rows = cross_ref[:, 0, row, :].astype(jnp.float32)
        imag_rows = cross_ref[:, 1, row, :].astype(jnp.float32)
        both = jnp.concatenate([real_rows, imag_rows], axis=0)
        out_ref[row] = jnp.dot(
            both.T.astype(jnp.bfloat16), table, preferred_element_type=jnp.float32
        )


def lag_transform(cross, table, interpret=False):
    freq_count, chan_count, pair_rows, block_width = cross.shape
    row_width = pair_rows // 2
    step_rows = 8 if row_width % 8 == 0 else row_width
    lag_count = table.shape[1]
    cross = cross.reshape(freq_count, chan_count, 2, row_width, block_width)
    return pl.pallas_call(
        lag_kernel,
        grid=(chan_count, row_width // step_rows),
        in_specs=[
            pl.BlockSpec(
                (freq_count, None, 2, step_rows, block_width), lambda c, h: (0, c, 0, h, 0)
            ),
            pl.BlockSpec((2 * freq_count, lag_count), lambda c, h: (0, 0)),
        ],
        out_specs=pl.BlockSpec((step_rows, block_width, lag_count), lambda c, h: (h, c, 0)),
        out_shape=jax.ShapeDtypeStruct((row_width, chan_count * block_width, lag_count), jnp.float32),
        interpret=interpret,
    )(cross, table)


def per_device(raw_samples):
    seg_count, block_width, raw_length = raw_samples.shape
    sample_count = raw_length // 2
    freq_count = sample_count // 8
    chan_count = lax.axis_size("chan")
    time_count = lax.axis_size("tm")
    channel_total = block_width * chan_count
    row_width = channel_total // (chan_count * time_count)
    raw_rows = raw_samples.reshape(seg_count * block_width, raw_length)
    folded = folded_tables(sample_count, freq_count)
    spectrum = jnp.dot(
        raw_rows, folded, precision=lax.Precision.HIGH, preferred_element_type=jnp.float32
    )
    real_part = spectrum[:, :freq_count].reshape(seg_count, block_width, freq_count)
    imag_part = spectrum[:, freq_count:].reshape(seg_count, block_width, freq_count)
    real_w, imag_w = whiten(real_part, imag_part)
    local_spec = jnp.stack([real_w, imag_w], axis=0).astype(jnp.bfloat16)
    local_spec = jnp.transpose(local_spec, (3, 0, 1, 2)).reshape(
        freq_count, 2 * seg_count, block_width
    )
    every = lax.all_gather(local_spec, ("chan", "tm"), axis=0)
    every = every.reshape(chan_count, time_count, freq_count, 2 * seg_count, block_width)
    chan_index = lax.axis_index("chan")
    tm_index = lax.axis_index("tm")
    own_block = lax.dynamic_index_in_dim(every, chan_index, 0, keepdims=False)
    row_ids = tm_index * row_width + jnp.arange(row_width, dtype=jnp.int32)
    pick = (jnp.arange(block_width, dtype=jnp.int32)[:, None] == row_ids[None, :])
    rows = jnp.einsum(
        "tkqw,wi->tkqi", own_block, pick.astype(jnp.bfloat16),
        preferred_element_type=jnp.float32,
    ).astype(jnp.bfloat16)
    rows = rows.reshape(time_count, freq_count, 2, seg_count, row_width)
    turned = jnp.stack([rows[:, :, 1], -rows[:, :, 0]], axis=2)
    left = jnp.concatenate([rows, turned], axis=4).reshape(
        time_count, freq_count, 2 * seg_count, 2 * row_width
    )
    norm_scale = 1.0 / math.sqrt(freq_count * seg_count * time_count)
    cross = jnp.einsum("tkqa,ctkqw->kcaw", left, every, preferred_element_type=jnp.float32)
    cross = (cross * norm_scale).astype(jnp.bfloat16)
    table = lag_table(freq_count, sample_count, LAGS)
    return lag_transform(cross, table)


def solution(mesh):
    return jax.shard_map(
        per_device,
        mesh=mesh,
        in_specs=(P("tm", "chan", None),),
        out_specs=P(("chan", "tm"), None, None),
        check_vma=False,
    )
```

```python
import math

import jax
import jax.numpy as jnp
from jax import lax
from jax.experimental import pallas as pl
from jax.sharding import PartitionSpec as P

LAGS = 256


def whiten(real_part, imag_part):
    power = real_part * real_part + imag_part * imag_part
    level = jnp.mean(power, axis=-1, keepdims=True)
    factor = 1.0 / jnp.sqrt(power + 0.1 * level + 1e-06)
    return (real_part * factor, imag_part * factor)


def lag_table(freq_count, sample_count, lag_count):
    freq_index = jnp.arange(1, freq_count + 1, dtype=jnp.int32)
    lag_index = jnp.arange(lag_count, dtype=jnp.int32) - lag_count // 2
    turns = freq_index[:, None] * (lag_index[None, :] % sample_count) % sample_count
    angle = turns.astype(jnp.float32) * (2.0 * math.pi / sample_count)
    return jnp.concatenate([jnp.cos(angle), -jnp.sin(angle)], axis=0).astype(jnp.bfloat16)


def folded_tables(sample_count, freq_count):
    fine_rows = 64
    coarse_rows = 2 * sample_count // fine_rows
    scale = 2.0 * math.pi / sample_count
    freq_index = jnp.arange(1, freq_count + 1, dtype=jnp.int32)[None, None, :]
    coarse_time = jnp.arange(coarse_rows, dtype=jnp.int32)[:, None, None] * (fine_rows // 2)
    fine = jnp.arange(fine_rows, dtype=jnp.int32)[None, :, None]
    fine_time = fine // 2
    odd = (fine % 2) == 1

    def angle(times):
        return (times * freq_index % sample_count).astype(jnp.float32) * scale

    coarse_angle = angle(coarse_time)
    coarse_cos, coarse_sin = jnp.cos(coarse_angle), jnp.sin(coarse_angle)
    this_angle = angle(fine_time)
    next_angle = angle(fine_time + 1)
    this_cos = coarse_cos * jnp.cos(this_angle) - coarse_sin * jnp.sin(this_angle)
    this_sin = coarse_sin * jnp.cos(this_angle) + coarse_cos * jnp.sin(this_angle)
    next_cos = coarse_cos * jnp.cos(next_angle) - coarse_sin * jnp.sin(next_angle)
    next_sin = coarse_sin * jnp.cos(next_angle) + coarse_cos * jnp.sin(next_angle)
    last_row = (coarse_time + fine_time + 1) >= sample_count
    this_weight = jnp.where(odd, 0.25, 0.5)
    next_weight = jnp.where(odd & ~last_row, 0.25, 0.0)
    cos_part = this_weight * this_cos + next_weight * next_cos
    sin_part = -(this_weight * this_sin + next_weight * next_sin)
    both = jnp.concatenate([cos_part, sin_part], axis=-1)
    return both.reshape(2 * sample_count, 2 * freq_count)


def lag_kernel(cross_ref, table_ref, out_ref):
    row_width = out_ref.shape[0]
    table = table_ref[...]
    for row in range(row_width):
        real_rows = cross_ref[:, row, :]
        imag_rows = cross_ref[:, row_width + row, :]
        both = jnp.concatenate([real_rows, imag_rows], axis=0)
        out_ref[row] = lax.dot_general(
            both, table, (((0,), (0,)), ((), ())), preferred_element_type=jnp.float32
        )


def lag_transform(cross, table, interpret=False):
    freq_count, chan_count, pair_rows, block_width = cross.shape
    row_width = pair_rows // 2
    lag_count = table.shape[1]
    return pl.pallas_call(
        lag_kernel,
        grid=(chan_count,),
        in_specs=[
            pl.BlockSpec((freq_count, None, pair_rows, block_width), lambda c: (0, c, 0, 0)),
            pl.BlockSpec((2 * freq_count, lag_count), lambda c: (0, 0)),
        ],
        out_specs=pl.BlockSpec((row_width, block_width, lag_count), lambda c: (0, c, 0)),
        out_shape=jax.ShapeDtypeStruct((row_width, chan_count * block_width, lag_count), jnp.float32),
        interpret=interpret,
    )(cross, table)


def per_device(raw_samples):
    seg_count, block_width, raw_length = raw_samples.shape
    sample_count = raw_length // 2
    freq_count = sample_count // 8
    chan_count = lax.axis_size("chan")
    time_count = lax.axis_size("tm")
    channel_total = block_width * chan_count
    row_width = channel_total // (chan_count * time_count)
    raw_rows = raw_samples.reshape(seg_count * block_width, raw_length)
    folded = folded_tables(sample_count, freq_count)
    spectrum = jnp.dot(
        raw_rows, folded, precision=lax.Precision.HIGH, preferred_element_type=jnp.float32
    )
    real_part = spectrum[:, :freq_count].reshape(seg_count, block_width, freq_count)
    imag_part = spectrum[:, freq_count:].reshape(seg_count, block_width, freq_count)
    real_w, imag_w = whiten(real_part, imag_part)
    local_spec = jnp.stack([real_w, imag_w], axis=0).astype(jnp.bfloat16)
    local_spec = jnp.transpose(local_spec, (3, 0, 1, 2)).reshape(
        freq_count, 2 * seg_count, block_width
    )
    every = lax.all_gather(local_spec, ("chan", "tm"), axis=0)
    every = every.reshape(chan_count, time_count, freq_count, 2 * seg_count, block_width)
    chan_index = lax.axis_index("chan")
    tm_index = lax.axis_index("tm")
    own_block = lax.dynamic_index_in_dim(every, chan_index, 0, keepdims=False)
    row_ids = tm_index * row_width + jnp.arange(row_width, dtype=jnp.int32)
    pick = (jnp.arange(block_width, dtype=jnp.int32)[:, None] == row_ids[None, :])
    rows = jnp.einsum(
        "tkqw,wi->tkqi", own_block, pick.astype(jnp.bfloat16),
        preferred_element_type=jnp.float32,
    ).astype(jnp.bfloat16)
    rows = rows.reshape(time_count, freq_count, 2, seg_count, row_width)
    turned = jnp.stack([rows[:, :, 1], -rows[:, :, 0]], axis=2)
    left = jnp.concatenate([rows, turned], axis=4).reshape(
        time_count, freq_count, 2 * seg_count, 2 * row_width
    )
    norm_scale = 1.0 / math.sqrt(freq_count * seg_count * time_count)
    cross = jnp.einsum("tkqa,ctkqw->kcaw", left, every, preferred_element_type=jnp.float32)
    cross = (cross * norm_scale).astype(jnp.bfloat16)
    table = lag_table(freq_count, sample_count, LAGS)
    return lag_transform(cross, table)


def solution(mesh):
    return jax.shard_map(
        per_device,
        mesh=mesh,
        in_specs=(P("tm", "chan", None),),
        out_specs=P(("chan", "tm"), None, None),
        check_vma=False,
    )
```

```python
import math

import jax
import jax.numpy as jnp
from jax import lax
from jax.experimental import pallas as pl
from jax.sharding import PartitionSpec as P

LAGS = 256


def whiten(real_part, imag_part):
    power = real_part * real_part + imag_part * imag_part
    level = jnp.mean(power, axis=-1, keepdims=True)
    factor = 1.0 / jnp.sqrt(power + 0.1 * level + 1e-06)
    return (real_part * factor, imag_part * factor)


def lag_table(freq_count, sample_count, lag_count):
    freq_index = jnp.arange(1, freq_count + 1, dtype=jnp.int32)
    lag_index = jnp.arange(lag_count, dtype=jnp.int32) - lag_count // 2
    turns = freq_index[:, None] * (lag_index[None, :] % sample_count) % sample_count
    angle = turns.astype(jnp.float32) * (2.0 * math.pi / sample_count)
    return jnp.concatenate([jnp.cos(angle), -jnp.sin(angle)], axis=0).astype(jnp.bfloat16)


def folded_tables(sample_count, freq_count):
    fine_rows = 64
    coarse_rows = 2 * sample_count // fine_rows
    scale = 2.0 * math.pi / sample_count
    freq_index = jnp.arange(1, freq_count + 1, dtype=jnp.int32)[None, None, :]
    coarse_time = jnp.arange(coarse_rows, dtype=jnp.int32)[:, None, None] * (fine_rows // 2)
    fine = jnp.arange(fine_rows, dtype=jnp.int32)[None, :, None]
    fine_time = fine // 2
    odd = (fine % 2) == 1

    def angle(times):
        return (times * freq_index % sample_count).astype(jnp.float32) * scale

    coarse_angle = angle(coarse_time)
    coarse_cos, coarse_sin = jnp.cos(coarse_angle), jnp.sin(coarse_angle)
    this_angle = angle(fine_time)
    next_angle = angle(fine_time + 1)
    this_cos = coarse_cos * jnp.cos(this_angle) - coarse_sin * jnp.sin(this_angle)
    this_sin = coarse_sin * jnp.cos(this_angle) + coarse_cos * jnp.sin(this_angle)
    next_cos = coarse_cos * jnp.cos(next_angle) - coarse_sin * jnp.sin(next_angle)
    next_sin = coarse_sin * jnp.cos(next_angle) + coarse_cos * jnp.sin(next_angle)
    last_row = (coarse_time + fine_time + 1) >= sample_count
    this_weight = jnp.where(odd, 0.25, 0.5)
    next_weight = jnp.where(odd & ~last_row, 0.25, 0.0)
    cos_part = this_weight * this_cos + next_weight * next_cos
    sin_part = -(this_weight * this_sin + next_weight * next_sin)
    both = jnp.concatenate([cos_part, sin_part], axis=-1)
    return both.reshape(2 * sample_count, 2 * freq_count)


def lag_kernel(cross_ref, table_ref, out_ref):
    row_width = out_ref.shape[0]
    table = table_ref[...]
    for row in range(row_width):
        real_rows = cross_ref[:, row, :]
        imag_rows = cross_ref[:, row_width + row, :]
        both = jnp.concatenate([real_rows, imag_rows], axis=0)
        out_ref[row] = lax.dot_general(
            both, table, (((0,), (0,)), ((), ())), preferred_element_type=jnp.float32
        )


def lag_transform(cross, table, interpret=False):
    freq_count, chan_count, pair_rows, block_width = cross.shape
    row_width = pair_rows // 2
    lag_count = table.shape[1]
    return pl.pallas_call(
        lag_kernel,
        grid=(chan_count,),
        in_specs=[
            pl.BlockSpec((freq_count, None, pair_rows, block_width), lambda c: (0, c, 0, 0)),
            pl.BlockSpec((2 * freq_count, lag_count), lambda c: (0, 0)),
        ],
        out_specs=pl.BlockSpec((row_width, block_width, lag_count), lambda c: (0, c, 0)),
        out_shape=jax.ShapeDtypeStruct((row_width, chan_count * block_width, lag_count), jnp.float32),
        interpret=interpret,
    )(cross, table)


def per_device(raw_samples):
    seg_count, block_width, raw_length = raw_samples.shape
    sample_count = raw_length // 2
    freq_count = sample_count // 8
    chan_count = lax.axis_size("chan")
    time_count = lax.axis_size("tm")
    channel_total = block_width * chan_count
    row_width = channel_total // (chan_count * time_count)
    raw_rows = raw_samples.reshape(seg_count * block_width, raw_length)
    folded = folded_tables(sample_count, freq_count)
    spectrum = jnp.dot(
        raw_rows, folded, precision=lax.Precision.HIGH, preferred_element_type=jnp.float32
    )
    real_part = spectrum[:, :freq_count].reshape(seg_count, block_width, freq_count)
    imag_part = spectrum[:, freq_count:].reshape(seg_count, block_width, freq_count)
    real_w, imag_w = whiten(real_part, imag_part)
    local_spec = jnp.stack([real_w, imag_w], axis=0).astype(jnp.bfloat16)
    local_spec = jnp.transpose(local_spec, (3, 0, 1, 2)).reshape(
        freq_count, 2 * seg_count, block_width
    )
    every = lax.all_gather(local_spec, ("chan", "tm"), axis=0)
    every = every.reshape(chan_count, time_count, freq_count, 2 * seg_count, block_width)
    chan_index = lax.axis_index("chan")
    tm_index = lax.axis_index("tm")
    parts = local_spec.reshape(freq_count, 2 * seg_count, time_count, row_width)
    parts = lax.all_to_all(parts, "tm", 2, 2, tiled=True)
    rows = jnp.transpose(parts, (2, 0, 1, 3))
    rows = rows.reshape(time_count, freq_count, 2, seg_count, row_width)
    turned = jnp.stack([rows[:, :, 1], -rows[:, :, 0]], axis=2)
    left = jnp.concatenate([rows, turned], axis=4).reshape(
        time_count, freq_count, 2 * seg_count, 2 * row_width
    )
    norm_scale = 1.0 / math.sqrt(freq_count * seg_count * time_count)
    cross = jnp.einsum("tkqa,ctkqw->kcaw", left, every, preferred_element_type=jnp.float32)
    cross = (cross * norm_scale).astype(jnp.bfloat16)
    table = lag_table(freq_count, sample_count, LAGS)
    return lag_transform(cross, table)


def solution(mesh):
    return jax.shard_map(
        per_device,
        mesh=mesh,
        in_specs=(P("tm", "chan", None),),
        out_specs=P(("chan", "tm"), None, None),
        check_vma=False,
    )
```

```python
import math

import jax
import jax.numpy as jnp
from jax import lax
from jax.experimental import pallas as pl
from jax.sharding import PartitionSpec as P

LAGS = 256


def whiten(real_part, imag_part):
    power = real_part * real_part + imag_part * imag_part
    level = jnp.mean(power, axis=-1, keepdims=True)
    factor = 1.0 / jnp.sqrt(power + 0.1 * level + 1e-06)
    return (real_part * factor, imag_part * factor)


def lag_table(freq_count, sample_count, lag_count):
    freq_index = jnp.arange(1, freq_count + 1, dtype=jnp.int32)
    lag_index = jnp.arange(lag_count, dtype=jnp.int32) - lag_count // 2
    turns = freq_index[:, None] * (lag_index[None, :] % sample_count) % sample_count
    angle = turns.astype(jnp.float32) * (2.0 * math.pi / sample_count)
    return jnp.concatenate([jnp.cos(angle), -jnp.sin(angle)], axis=0).astype(jnp.bfloat16)


def folded_tables(sample_count, freq_count):
    fine_rows = 64
    coarse_rows = 2 * sample_count // fine_rows
    scale = 2.0 * math.pi / sample_count
    freq_index = jnp.arange(1, freq_count + 1, dtype=jnp.int32)[None, None, :]
    coarse_time = jnp.arange(coarse_rows, dtype=jnp.int32)[:, None, None] * (fine_rows // 2)
    fine = jnp.arange(fine_rows, dtype=jnp.int32)[None, :, None]
    fine_time = fine // 2
    odd = (fine % 2) == 1

    def angle(times):
        return (times * freq_index % sample_count).astype(jnp.float32) * scale

    coarse_angle = angle(coarse_time)
    coarse_cos, coarse_sin = jnp.cos(coarse_angle), jnp.sin(coarse_angle)
    this_angle = angle(fine_time)
    next_angle = angle(fine_time + 1)
    this_cos = coarse_cos * jnp.cos(this_angle) - coarse_sin * jnp.sin(this_angle)
    this_sin = coarse_sin * jnp.cos(this_angle) + coarse_cos * jnp.sin(this_angle)
    next_cos = coarse_cos * jnp.cos(next_angle) - coarse_sin * jnp.sin(next_angle)
    next_sin = coarse_sin * jnp.cos(next_angle) + coarse_cos * jnp.sin(next_angle)
    last_row = (coarse_time + fine_time + 1) >= sample_count
    this_weight = jnp.where(odd, 0.25, 0.5)
    next_weight = jnp.where(odd & ~last_row, 0.25, 0.0)
    cos_part = this_weight * this_cos + next_weight * next_cos
    sin_part = -(this_weight * this_sin + next_weight * next_sin)
    both = jnp.concatenate([cos_part, sin_part], axis=-1)
    return both.reshape(2 * sample_count, 2 * freq_count)


def lag_kernel(cross_ref, table_ref, out_ref):
    row_width = out_ref.shape[0]
    block_count = cross_ref.shape[1]
    block_width = cross_ref.shape[3]
    table = table_ref[...]
    for block in range(block_count):
        for row in range(row_width):
            real_rows = cross_ref[:, block, row, :]
            imag_rows = cross_ref[:, block, row_width + row, :]
            both = jnp.concatenate([real_rows, imag_rows], axis=0)
            out_ref[row, block * block_width:(block + 1) * block_width, :] = lax.dot_general(
                both, table, (((0,), (0,)), ((), ())), preferred_element_type=jnp.float32
            )


def lag_transform(cross, table, interpret=False):
    freq_count, chan_count, pair_rows, block_width = cross.shape
    row_width = pair_rows // 2
    step_blocks = 2 if chan_count % 2 == 0 else 1
    lag_count = table.shape[1]
    return pl.pallas_call(
        lag_kernel,
        grid=(chan_count // step_blocks,),
        in_specs=[
            pl.BlockSpec((freq_count, step_blocks, pair_rows, block_width), lambda c: (0, c, 0, 0)),
            pl.BlockSpec((2 * freq_count, lag_count), lambda c: (0, 0)),
        ],
        out_specs=pl.BlockSpec(
            (row_width, step_blocks * block_width, lag_count), lambda c: (0, c, 0)
        ),
        out_shape=jax.ShapeDtypeStruct((row_width, chan_count * block_width, lag_count), jnp.float32),
        interpret=interpret,
    )(cross, table)


def per_device(raw_samples):
    seg_count, block_width, raw_length = raw_samples.shape
    sample_count = raw_length // 2
    freq_count = sample_count // 8
    chan_count = lax.axis_size("chan")
    time_count = lax.axis_size("tm")
    channel_total = block_width * chan_count
    row_width = channel_total // (chan_count * time_count)
    raw_rows = raw_samples.reshape(seg_count * block_width, raw_length)
    folded = folded_tables(sample_count, freq_count)
    spectrum = jnp.dot(
        raw_rows, folded, precision=lax.Precision.HIGH, preferred_element_type=jnp.float32
    )
    real_part = spectrum[:, :freq_count].reshape(seg_count, block_width, freq_count)
    imag_part = spectrum[:, freq_count:].reshape(seg_count, block_width, freq_count)
    real_w, imag_w = whiten(real_part, imag_part)
    local_spec = jnp.stack([real_w, imag_w], axis=0).astype(jnp.bfloat16)
    local_spec = jnp.transpose(local_spec, (3, 0, 1, 2)).reshape(
        freq_count, 2 * seg_count, block_width
    )
    every = lax.all_gather(local_spec, ("chan", "tm"), axis=0)
    every = every.reshape(chan_count, time_count, freq_count, 2 * seg_count, block_width)
    chan_index = lax.axis_index("chan")
    tm_index = lax.axis_index("tm")
    parts = local_spec.reshape(freq_count, 2 * seg_count, time_count, row_width)
    parts = lax.all_to_all(parts, "tm", 2, 2, tiled=True)
    rows = jnp.transpose(parts, (2, 0, 1, 3))
    rows = rows.reshape(time_count, freq_count, 2, seg_count, row_width)
    turned = jnp.stack([rows[:, :, 1], -rows[:, :, 0]], axis=2)
    left = jnp.concatenate([rows, turned], axis=4).reshape(
        time_count, freq_count, 2 * seg_count, 2 * row_width
    )
    norm_scale = 1.0 / math.sqrt(freq_count * seg_count * time_count)
    cross = jnp.einsum("tkqa,ctkqw->kcaw", left, every, preferred_element_type=jnp.float32)
    cross = (cross * norm_scale).astype(jnp.bfloat16)
    table = lag_table(freq_count, sample_count, LAGS)
    return lag_transform(cross, table)


def solution(mesh):
    return jax.shard_map(
        per_device,
        mesh=mesh,
        in_specs=(P("tm", "chan", None),),
        out_specs=P(("chan", "tm"), None, None),
        check_vma=False,
    )
```

```python
import math

import jax
import jax.numpy as jnp
from jax import lax
from jax.experimental import pallas as pl
from jax.sharding import PartitionSpec as P

LAGS = 256


def whiten(real_part, imag_part):
    power = real_part * real_part + imag_part * imag_part
    level = jnp.mean(power, axis=-1, keepdims=True)
    factor = 1.0 / jnp.sqrt(power + 0.1 * level + 1e-06)
    return (real_part * factor, imag_part * factor)


def lag_table(freq_count, sample_count, lag_count):
    freq_index = jnp.arange(1, freq_count + 1, dtype=jnp.int32)
    lag_index = jnp.arange(lag_count, dtype=jnp.int32) - lag_count // 2
    turns = freq_index[:, None] * (lag_index[None, :] % sample_count) % sample_count
    angle = turns.astype(jnp.float32) * (2.0 * math.pi / sample_count)
    return jnp.concatenate([jnp.cos(angle), -jnp.sin(angle)], axis=0).astype(jnp.bfloat16)


def folded_tables(sample_count, freq_count):
    fine_rows = 64
    coarse_rows = 2 * sample_count // fine_rows
    scale = 2.0 * math.pi / sample_count
    freq_index = jnp.arange(1, freq_count + 1, dtype=jnp.int32)[None, None, :]
    coarse_time = jnp.arange(coarse_rows, dtype=jnp.int32)[:, None, None] * (fine_rows // 2)
    fine = jnp.arange(fine_rows, dtype=jnp.int32)[None, :, None]
    fine_time = fine // 2
    odd = (fine % 2) == 1

    def angle(times):
        return (times * freq_index % sample_count).astype(jnp.float32) * scale

    coarse_angle = angle(coarse_time)
    coarse_cos, coarse_sin = jnp.cos(coarse_angle), jnp.sin(coarse_angle)
    this_angle = angle(fine_time)
    next_angle = angle(fine_time + 1)
    this_cos = coarse_cos * jnp.cos(this_angle) - coarse_sin * jnp.sin(this_angle)
    this_sin = coarse_sin * jnp.cos(this_angle) + coarse_cos * jnp.sin(this_angle)
    next_cos = coarse_cos * jnp.cos(next_angle) - coarse_sin * jnp.sin(next_angle)
    next_sin = coarse_sin * jnp.cos(next_angle) + coarse_cos * jnp.sin(next_angle)
    last_row = (coarse_time + fine_time + 1) >= sample_count
    this_weight = jnp.where(odd, 0.25, 0.5)
    next_weight = jnp.where(odd & ~last_row, 0.25, 0.0)
    cos_part = this_weight * this_cos + next_weight * next_cos
    sin_part = -(this_weight * this_sin + next_weight * next_sin)
    both = jnp.concatenate([cos_part, sin_part], axis=-1)
    return both.reshape(2 * sample_count, 2 * freq_count)


def lag_kernel(cross_ref, table_ref, out_ref):
    row_width = out_ref.shape[0]
    block_count = cross_ref.shape[1]
    block_width = cross_ref.shape[3]
    table = table_ref[...]
    pair = 2 if row_width % 2 == 0 else 1
    for block in range(block_count):
        for first in range(0, row_width, pair):
            both = jnp.concatenate(
                [
                    jnp.concatenate(
                        [cross_ref[:, block, row, :], cross_ref[:, block, row_width + row, :]],
                        axis=0,
                    )
                    for row in range(first, first + pair)
                ],
                axis=1,
            )
            lags = lax.dot_general(
                both, table, (((0,), (0,)), ((), ())), preferred_element_type=jnp.float32
            )
            for offset in range(pair):
                out_ref[first + offset, block * block_width:(block + 1) * block_width, :] = lags[
                    offset * block_width:(offset + 1) * block_width
                ]


def lag_transform(cross, table, interpret=False):
    freq_count, chan_count, pair_rows, block_width = cross.shape
    row_width = pair_rows // 2
    step_blocks = 2 if chan_count % 2 == 0 else 1
    lag_count = table.shape[1]
    return pl.pallas_call(
        lag_kernel,
        grid=(chan_count // step_blocks,),
        in_specs=[
            pl.BlockSpec((freq_count, step_blocks, pair_rows, block_width), lambda c: (0, c, 0, 0)),
            pl.BlockSpec((2 * freq_count, lag_count), lambda c: (0, 0)),
        ],
        out_specs=pl.BlockSpec(
            (row_width, step_blocks * block_width, lag_count), lambda c: (0, c, 0)
        ),
        out_shape=jax.ShapeDtypeStruct((row_width, chan_count * block_width, lag_count), jnp.float32),
        interpret=interpret,
    )(cross, table)


def per_device(raw_samples):
    seg_count, block_width, raw_length = raw_samples.shape
    sample_count = raw_length // 2
    freq_count = sample_count // 8
    chan_count = lax.axis_size("chan")
    time_count = lax.axis_size("tm")
    channel_total = block_width * chan_count
    row_width = channel_total // (chan_count * time_count)
    raw_rows = raw_samples.reshape(seg_count * block_width, raw_length)
    folded = folded_tables(sample_count, freq_count)
    spectrum = jnp.dot(
        raw_rows, folded, precision=lax.Precision.HIGH, preferred_element_type=jnp.float32
    )
    real_part = spectrum[:, :freq_count].reshape(seg_count, block_width, freq_count)
    imag_part = spectrum[:, freq_count:].reshape(seg_count, block_width, freq_count)
    real_w, imag_w = whiten(real_part, imag_part)
    local_spec = jnp.stack([real_w, imag_w], axis=0).astype(jnp.bfloat16)
    local_spec = jnp.transpose(local_spec, (3, 0, 1, 2)).reshape(
        freq_count, 2 * seg_count, block_width
    )
    every = lax.all_gather(local_spec, ("chan", "tm"), axis=0)
    every = every.reshape(chan_count, time_count, freq_count, 2 * seg_count, block_width)
    chan_index = lax.axis_index("chan")
    tm_index = lax.axis_index("tm")
    parts = local_spec.reshape(freq_count, 2 * seg_count, time_count, row_width)
    parts = lax.all_to_all(parts, "tm", 2, 2, tiled=True)
    rows = jnp.transpose(parts, (2, 0, 1, 3))
    rows = rows.reshape(time_count, freq_count, 2, seg_count, row_width)
    turned = jnp.stack([rows[:, :, 1], -rows[:, :, 0]], axis=2)
    left = jnp.concatenate([rows, turned], axis=4).reshape(
        time_count, freq_count, 2 * seg_count, 2 * row_width
    )
    norm_scale = 1.0 / math.sqrt(freq_count * seg_count * time_count)
    cross = jnp.einsum("tkqa,ctkqw->kcaw", left, every, preferred_element_type=jnp.float32)
    cross = (cross * norm_scale).astype(jnp.bfloat16)
    table = lag_table(freq_count, sample_count, LAGS)
    return lag_transform(cross, table)


def solution(mesh):
    return jax.shard_map(
        per_device,
        mesh=mesh,
        in_specs=(P("tm", "chan", None),),
        out_specs=P(("chan", "tm"), None, None),
        check_vma=False,
    )
```

```python
import math

import numpy as np

import jax
import jax.numpy as jnp
from jax import lax
from jax.experimental import pallas as pl
from jax.sharding import PartitionSpec as P

LAGS = 256


def whiten(real_part, imag_part):
    power = real_part * real_part + imag_part * imag_part
    level = jnp.mean(power, axis=-1, keepdims=True)
    factor = 1.0 / jnp.sqrt(power + 0.1 * level + 1e-06)
    return (real_part * factor, imag_part * factor)


def lag_table(freq_count, sample_count, lag_count):
    freq_index = jnp.arange(1, freq_count + 1, dtype=jnp.int32)
    lag_index = jnp.arange(lag_count, dtype=jnp.int32) - lag_count // 2
    turns = freq_index[:, None] * (lag_index[None, :] % sample_count) % sample_count
    angle = turns.astype(jnp.float32) * (2.0 * math.pi / sample_count)
    return jnp.concatenate([jnp.cos(angle), -jnp.sin(angle)], axis=0).astype(jnp.bfloat16)


def folded_tables(sample_count, freq_count):
    time_index = np.arange(sample_count + 1, dtype=np.int64)[:, None]
    freq_index = np.arange(1, freq_count + 1, dtype=np.int64)[None, :]
    angle = (time_index * freq_index % sample_count) * (2.0 * np.pi / sample_count)
    table = np.concatenate([np.cos(angle), -np.sin(angle)], axis=1)
    table[sample_count] = 0.0
    folded = np.empty((2 * sample_count, 2 * freq_count))
    folded[0::2] = 0.5 * table[:sample_count]
    folded[1::2] = 0.25 * table[:sample_count] + 0.25 * table[1:]
    return jnp.asarray(folded.astype(np.float32))


def lag_kernel(cross_ref, table_ref, out_ref):
    row_width = out_ref.shape[0]
    block_count = cross_ref.shape[1]
    block_width = cross_ref.shape[3]
    table = table_ref[...]
    for block in range(block_count):
        for row in range(row_width):
            real_rows = cross_ref[:, block, row, :]
            imag_rows = cross_ref[:, block, row_width + row, :]
            both = jnp.concatenate([real_rows, imag_rows], axis=0)
            out_ref[row, block * block_width:(block + 1) * block_width, :] = lax.dot_general(
                both, table, (((0,), (0,)), ((), ())), preferred_element_type=jnp.float32
            )


def lag_transform(cross, table, interpret=False):
    freq_count, chan_count, pair_rows, block_width = cross.shape
    row_width = pair_rows // 2
    step_blocks = 2 if chan_count % 2 == 0 else 1
    lag_count = table.shape[1]
    return pl.pallas_call(
        lag_kernel,
        grid=(chan_count // step_blocks,),
        in_specs=[
            pl.BlockSpec((freq_count, step_blocks, pair_rows, block_width), lambda c: (0, c, 0, 0)),
            pl.BlockSpec((2 * freq_count, lag_count), lambda c: (0, 0)),
        ],
        out_specs=pl.BlockSpec(
            (row_width, step_blocks * block_width, lag_count), lambda c: (0, c, 0)
        ),
        out_shape=jax.ShapeDtypeStruct((row_width, chan_count * block_width, lag_count), jnp.float32),
        interpret=interpret,
    )(cross, table)


def per_device(raw_samples):
    seg_count, block_width, raw_length = raw_samples.shape
    sample_count = raw_length // 2
    freq_count = sample_count // 8
    chan_count = lax.axis_size("chan")
    time_count = lax.axis_size("tm")
    channel_total = block_width * chan_count
    row_width = channel_total // (chan_count * time_count)
    raw_rows = raw_samples.reshape(seg_count * block_width, raw_length)
    folded = folded_tables(sample_count, freq_count)
    spectrum = jnp.dot(
        raw_rows, folded, precision=lax.Precision.HIGH, preferred_element_type=jnp.float32
    )
    real_part = spectrum[:, :freq_count].reshape(seg_count, block_width, freq_count)
    imag_part = spectrum[:, freq_count:].reshape(seg_count, block_width, freq_count)
    real_w, imag_w = whiten(real_part, imag_part)
    local_spec = jnp.stack([real_w, imag_w], axis=0).astype(jnp.bfloat16)
    local_spec = jnp.transpose(local_spec, (3, 0, 1, 2)).reshape(
        freq_count, 2 * seg_count, block_width
    )
    every = lax.all_gather(local_spec, ("chan", "tm"), axis=0)
    every = every.reshape(chan_count, time_count, freq_count, 2 * seg_count, block_width)
    chan_index = lax.axis_index("chan")
    tm_index = lax.axis_index("tm")
    parts = local_spec.reshape(freq_count, 2 * seg_count, time_count, row_width)
    parts = lax.all_to_all(parts, "tm", 2, 2, tiled=True)
    rows = jnp.transpose(parts, (2, 0, 1, 3))
    rows = rows.reshape(time_count, freq_count, 2, seg_count, row_width)
    turned = jnp.stack([rows[:, :, 1], -rows[:, :, 0]], axis=2)
    left = jnp.concatenate([rows, turned], axis=4).reshape(
        time_count, freq_count, 2 * seg_count, 2 * row_width
    )
    norm_scale = 1.0 / math.sqrt(freq_count * seg_count * time_count)
    cross = jnp.einsum("tkqa,ctkqw->kcaw", left, every, preferred_element_type=jnp.float32)
    cross = (cross * norm_scale).astype(jnp.bfloat16)
    table = lag_table(freq_count, sample_count, LAGS)
    return lag_transform(cross, table)


def solution(mesh):
    return jax.shard_map(
        per_device,
        mesh=mesh,
        in_specs=(P("tm", "chan", None),),
        out_specs=P(("chan", "tm"), None, None),
        check_vma=False,
    )
```

```python
import math

import ml_dtypes
import numpy as np

import jax
import jax.numpy as jnp
from jax import lax
from jax.experimental import pallas as pl
from jax.sharding import PartitionSpec as P

LAGS = 256


def whiten(real_part, imag_part):
    power = real_part * real_part + imag_part * imag_part
    level = jnp.mean(power, axis=-1, keepdims=True)
    factor = 1.0 / jnp.sqrt(power + 0.1 * level + 1e-06)
    return (real_part * factor, imag_part * factor)


def lag_table(freq_count, sample_count, lag_count):
    freq_index = jnp.arange(1, freq_count + 1, dtype=jnp.int32)
    lag_index = jnp.arange(lag_count, dtype=jnp.int32) - lag_count // 2
    turns = freq_index[:, None] * (lag_index[None, :] % sample_count) % sample_count
    angle = turns.astype(jnp.float32) * (2.0 * math.pi / sample_count)
    return jnp.concatenate([jnp.cos(angle), -jnp.sin(angle)], axis=0).astype(jnp.bfloat16)


def folded_tables(sample_count, freq_count):
    time_index = np.arange(sample_count + 1, dtype=np.int64)[:, None]
    freq_index = np.arange(1, freq_count + 1, dtype=np.int64)[None, :]
    angle = (time_index * freq_index % sample_count) * (2.0 * np.pi / sample_count)
    table = np.concatenate([np.cos(angle), -np.sin(angle)], axis=1)
    table[sample_count] = 0.0
    folded = np.empty((2 * sample_count, 2 * freq_count))
    folded[0::2] = 0.5 * table[:sample_count]
    folded[1::2] = 0.25 * table[:sample_count] + 0.25 * table[1:]
    head = folded.astype(np.float32).astype(ml_dtypes.bfloat16)
    tail = (folded - head.astype(np.float64)).astype(np.float32).astype(ml_dtypes.bfloat16)
    return jnp.asarray(head), jnp.asarray(tail)


def lag_kernel(cross_ref, table_ref, out_ref):
    row_width = out_ref.shape[0]
    block_count = cross_ref.shape[1]
    block_width = cross_ref.shape[3]
    table = table_ref[...]
    for block in range(block_count):
        for row in range(row_width):
            real_rows = cross_ref[:, block, row, :]
            imag_rows = cross_ref[:, block, row_width + row, :]
            both = jnp.concatenate([real_rows, imag_rows], axis=0)
            out_ref[row, block * block_width:(block + 1) * block_width, :] = lax.dot_general(
                both, table, (((0,), (0,)), ((), ())), preferred_element_type=jnp.float32
            )


def lag_transform(cross, table, interpret=False):
    freq_count, chan_count, pair_rows, block_width = cross.shape
    row_width = pair_rows // 2
    step_blocks = 2 if chan_count % 2 == 0 else 1
    lag_count = table.shape[1]
    return pl.pallas_call(
        lag_kernel,
        grid=(chan_count // step_blocks,),
        in_specs=[
            pl.BlockSpec((freq_count, step_blocks, pair_rows, block_width), lambda c: (0, c, 0, 0)),
            pl.BlockSpec((2 * freq_count, lag_count), lambda c: (0, 0)),
        ],
        out_specs=pl.BlockSpec(
            (row_width, step_blocks * block_width, lag_count), lambda c: (0, c, 0)
        ),
        out_shape=jax.ShapeDtypeStruct((row_width, chan_count * block_width, lag_count), jnp.float32),
        interpret=interpret,
    )(cross, table)


def per_device(raw_samples):
    seg_count, block_width, raw_length = raw_samples.shape
    sample_count = raw_length // 2
    freq_count = sample_count // 8
    chan_count = lax.axis_size("chan")
    time_count = lax.axis_size("tm")
    channel_total = block_width * chan_count
    row_width = channel_total // (chan_count * time_count)
    raw_rows = raw_samples.reshape(seg_count * block_width, raw_length)
    table_head, table_tail = folded_tables(sample_count, freq_count)
    raw_head = raw_rows.astype(jnp.bfloat16)
    raw_tail = (raw_rows - raw_head.astype(jnp.float32)).astype(jnp.bfloat16)
    spectrum = (
        jnp.dot(raw_head, table_head, preferred_element_type=jnp.float32)
        + jnp.dot(raw_head, table_tail, preferred_element_type=jnp.float32)
        + jnp.dot(raw_tail, table_head, preferred_element_type=jnp.float32)
    )
    real_part = spectrum[:, :freq_count].reshape(seg_count, block_width, freq_count)
    imag_part = spectrum[:, freq_count:].reshape(seg_count, block_width, freq_count)
    real_w, imag_w = whiten(real_part, imag_part)
    local_spec = jnp.stack([real_w, imag_w], axis=0).astype(jnp.bfloat16)
    local_spec = jnp.transpose(local_spec, (3, 0, 1, 2)).reshape(
        freq_count, 2 * seg_count, block_width
    )
    every = lax.all_gather(local_spec, ("chan", "tm"), axis=0)
    every = every.reshape(chan_count, time_count, freq_count, 2 * seg_count, block_width)
    chan_index = lax.axis_index("chan")
    tm_index = lax.axis_index("tm")
    parts = local_spec.reshape(freq_count, 2 * seg_count, time_count, row_width)
    parts = lax.all_to_all(parts, "tm", 2, 2, tiled=True)
    rows = jnp.transpose(parts, (2, 0, 1, 3))
    rows = rows.reshape(time_count, freq_count, 2, seg_count, row_width)
    turned = jnp.stack([rows[:, :, 1], -rows[:, :, 0]], axis=2)
    left = jnp.concatenate([rows, turned], axis=4).reshape(
        time_count, freq_count, 2 * seg_count, 2 * row_width
    )
    norm_scale = 1.0 / math.sqrt(freq_count * seg_count * time_count)
    cross = jnp.einsum("tkqa,ctkqw->kcaw", left, every, preferred_element_type=jnp.float32)
    cross = (cross * norm_scale).astype(jnp.bfloat16)
    table = lag_table(freq_count, sample_count, LAGS)
    return lag_transform(cross, table)


def solution(mesh):
    return jax.shard_map(
        per_device,
        mesh=mesh,
        in_specs=(P("tm", "chan", None),),
        out_specs=P(("chan", "tm"), None, None),
        check_vma=False,
    )
```

```python
import math

import numpy as np

import jax
import jax.numpy as jnp
from jax import lax
from jax.experimental import pallas as pl
from jax.sharding import PartitionSpec as P

LAGS = 256


def whiten(real_part, imag_part):
    power = real_part * real_part + imag_part * imag_part
    level = jnp.mean(power, axis=-1, keepdims=True)
    factor = 1.0 / jnp.sqrt(power + 0.1 * level + 1e-06)
    return (real_part * factor, imag_part * factor)


def lag_table(freq_count, sample_count, lag_count):
    freq_index = jnp.arange(1, freq_count + 1, dtype=jnp.int32)
    lag_index = jnp.arange(lag_count, dtype=jnp.int32) - lag_count // 2
    turns = freq_index[:, None] * (lag_index[None, :] % sample_count) % sample_count
    angle = turns.astype(jnp.float32) * (2.0 * math.pi / sample_count)
    return jnp.concatenate([jnp.cos(angle), -jnp.sin(angle)], axis=0).astype(jnp.bfloat16)


def folded_tables(sample_count, freq_count):
    time_index = np.arange(sample_count + 1, dtype=np.int64)[:, None]
    freq_index = np.arange(1, freq_count + 1, dtype=np.int64)[None, :]
    angle = (time_index * freq_index % sample_count) * (2.0 * np.pi / sample_count)
    table = np.concatenate([np.cos(angle), -np.sin(angle)], axis=1)
    table[sample_count] = 0.0
    folded = np.empty((2 * sample_count, 2 * freq_count))
    folded[0::2] = 0.5 * table[:sample_count]
    folded[1::2] = 0.25 * table[:sample_count] + 0.25 * table[1:]
    return jnp.asarray(folded.astype(np.float32))


def lag_kernel(cross_ref, table_ref, out_ref):
    row_width = out_ref.shape[0]
    block_count = cross_ref.shape[1]
    block_width = cross_ref.shape[3]
    table = table_ref[...]
    for block in range(block_count):
        for row in range(row_width):
            real_rows = cross_ref[:, block, row, :]
            imag_rows = cross_ref[:, block, row_width + row, :]
            both = jnp.concatenate([real_rows, imag_rows], axis=0).astype(jnp.bfloat16)
            out_ref[row, block * block_width:(block + 1) * block_width, :] = lax.dot_general(
                both, table, (((0,), (0,)), ((), ())), preferred_element_type=jnp.float32
            )


def lag_transform(cross, table, interpret=False):
    freq_count, chan_count, pair_rows, block_width = cross.shape
    row_width = pair_rows // 2
    step_blocks = 2 if chan_count % 2 == 0 else 1
    lag_count = table.shape[1]
    return pl.pallas_call(
        lag_kernel,
        grid=(chan_count // step_blocks,),
        in_specs=[
            pl.BlockSpec((freq_count, step_blocks, pair_rows, block_width), lambda c: (0, c, 0, 0)),
            pl.BlockSpec((2 * freq_count, lag_count), lambda c: (0, 0)),
        ],
        out_specs=pl.BlockSpec(
            (row_width, step_blocks * block_width, lag_count), lambda c: (0, c, 0)
        ),
        out_shape=jax.ShapeDtypeStruct((row_width, chan_count * block_width, lag_count), jnp.float32),
        interpret=interpret,
    )(cross, table)


def per_device(raw_samples):
    seg_count, block_width, raw_length = raw_samples.shape
    sample_count = raw_length // 2
    freq_count = sample_count // 8
    chan_count = lax.axis_size("chan")
    time_count = lax.axis_size("tm")
    channel_total = block_width * chan_count
    row_width = channel_total // (chan_count * time_count)
    raw_rows = raw_samples.reshape(seg_count * block_width, raw_length)
    folded = folded_tables(sample_count, freq_count)
    spectrum = jnp.dot(
        raw_rows, folded, precision=lax.Precision.HIGH, preferred_element_type=jnp.float32
    )
    real_part = spectrum[:, :freq_count].reshape(seg_count, block_width, freq_count)
    imag_part = spectrum[:, freq_count:].reshape(seg_count, block_width, freq_count)
    real_w, imag_w = whiten(real_part, imag_part)
    local_spec = jnp.stack([real_w, imag_w], axis=0).astype(jnp.bfloat16)
    local_spec = jnp.transpose(local_spec, (3, 0, 1, 2)).reshape(
        freq_count, 2 * seg_count, block_width
    )
    every = lax.all_gather(local_spec, ("chan", "tm"), axis=0)
    every = every.reshape(chan_count, time_count, freq_count, 2 * seg_count, block_width)
    chan_index = lax.axis_index("chan")
    tm_index = lax.axis_index("tm")
    parts = local_spec.reshape(freq_count, 2 * seg_count, time_count, row_width)
    parts = lax.all_to_all(parts, "tm", 2, 2, tiled=True)
    rows = jnp.transpose(parts, (2, 0, 1, 3))
    rows = rows.reshape(time_count, freq_count, 2, seg_count, row_width)
    turned = jnp.stack([rows[:, :, 1], -rows[:, :, 0]], axis=2)
    left = jnp.concatenate([rows, turned], axis=4).reshape(
        time_count, freq_count, 2 * seg_count, 2 * row_width
    )
    norm_scale = 1.0 / math.sqrt(freq_count * seg_count * time_count)
    cross = jnp.einsum("tkqa,ctkqw->kcaw", left, every, preferred_element_type=jnp.float32)
    cross = cross * norm_scale
    table = lag_table(freq_count, sample_count, LAGS)
    return lag_transform(cross, table)


def solution(mesh):
    return jax.shard_map(
        per_device,
        mesh=mesh,
        in_specs=(P("tm", "chan", None),),
        out_specs=P(("chan", "tm"), None, None),
        check_vma=False,
    )
```

```python
import math

import numpy as np

import jax
import jax.numpy as jnp
from jax import lax
from jax.experimental import pallas as pl
from jax.sharding import PartitionSpec as P

LAGS = 256


def whiten(real_part, imag_part):
    power = real_part * real_part + imag_part * imag_part
    level = jnp.mean(power, axis=-1, keepdims=True)
    factor = 1.0 / jnp.sqrt(power + 0.1 * level + 1e-06)
    return (real_part * factor, imag_part * factor)


def lag_table(freq_count, sample_count, lag_count):
    freq_index = jnp.arange(1, freq_count + 1, dtype=jnp.int32)
    lag_index = jnp.arange(lag_count, dtype=jnp.int32) - lag_count // 2
    turns = freq_index[:, None] * (lag_index[None, :] % sample_count) % sample_count
    angle = turns.astype(jnp.float32) * (2.0 * math.pi / sample_count)
    return jnp.concatenate([jnp.cos(angle), -jnp.sin(angle)], axis=0).astype(jnp.bfloat16)


def folded_tables(sample_count, freq_count):
    time_index = np.arange(sample_count + 1, dtype=np.int64)[:, None]
    freq_index = np.arange(1, freq_count + 1, dtype=np.int64)[None, :]
    angle = (time_index * freq_index % sample_count) * (2.0 * np.pi / sample_count)
    table = np.concatenate([np.cos(angle), -np.sin(angle)], axis=1)
    table[sample_count] = 0.0
    folded = np.empty((2 * sample_count, 2 * freq_count))
    folded[0::2] = 0.5 * table[:sample_count]
    folded[1::2] = 0.25 * table[:sample_count] + 0.25 * table[1:]
    return jnp.asarray(folded.astype(np.float32))


def lag_kernel(cross_ref, table_ref, out_ref):
    row_width = out_ref.shape[0]
    block_count = cross_ref.shape[1]
    block_width = cross_ref.shape[3]
    table = table_ref[...]
    for block in range(block_count):
        for row in range(row_width):
            real_rows = cross_ref[:, block, row, :]
            imag_rows = cross_ref[:, block, row_width + row, :]
            both = jnp.concatenate([real_rows, imag_rows], axis=0)
            out_ref[row, block * block_width:(block + 1) * block_width, :] = lax.dot_general(
                both, table, (((0,), (0,)), ((), ())), preferred_element_type=jnp.float32
            )


def lag_transform(cross, table, interpret=False):
    freq_count, chan_count, pair_rows, block_width = cross.shape
    row_width = pair_rows // 2
    step_blocks = 2 if chan_count % 2 == 0 else 1
    lag_count = table.shape[1]
    return pl.pallas_call(
        lag_kernel,
        grid=(chan_count // step_blocks,),
        in_specs=[
            pl.BlockSpec((freq_count, step_blocks, pair_rows, block_width), lambda c: (0, c, 0, 0)),
            pl.BlockSpec((2 * freq_count, lag_count), lambda c: (0, 0)),
        ],
        out_specs=pl.BlockSpec(
            (row_width, step_blocks * block_width, lag_count), lambda c: (0, c, 0)
        ),
        out_shape=jax.ShapeDtypeStruct((row_width, chan_count * block_width, lag_count), jnp.float32),
        interpret=interpret,
    )(cross, table)


def per_device(raw_samples):
    seg_count, block_width, raw_length = raw_samples.shape
    sample_count = raw_length // 2
    freq_count = sample_count // 8
    chan_count = lax.axis_size("chan")
    time_count = lax.axis_size("tm")
    channel_total = block_width * chan_count
    row_width = channel_total // (chan_count * time_count)
    raw_rows = raw_samples.reshape(seg_count * block_width, raw_length)
    folded = folded_tables(sample_count, freq_count)
    spectrum = jnp.einsum(
        "nk,rn->kr", folded, raw_rows, precision=lax.Precision.HIGH,
        preferred_element_type=jnp.float32,
    )
    real_part = spectrum[:freq_count].reshape(freq_count, seg_count, block_width)
    imag_part = spectrum[freq_count:].reshape(freq_count, seg_count, block_width)
    power = real_part * real_part + imag_part * imag_part
    level = jnp.mean(power, axis=0, keepdims=True)
    factor = 1.0 / jnp.sqrt(power + 0.1 * level + 1e-06)
    local_spec = jnp.stack([real_part * factor, imag_part * factor], axis=1).astype(jnp.bfloat16)
    local_spec = local_spec.reshape(freq_count, 2 * seg_count, block_width)
    every = lax.all_gather(local_spec, ("chan", "tm"), axis=0)
    every = every.reshape(chan_count, time_count, freq_count, 2 * seg_count, block_width)
    chan_index = lax.axis_index("chan")
    tm_index = lax.axis_index("tm")
    parts = local_spec.reshape(freq_count, 2 * seg_count, time_count, row_width)
    parts = lax.all_to_all(parts, "tm", 2, 2, tiled=True)
    rows = jnp.transpose(parts, (2, 0, 1, 3))
    rows = rows.reshape(time_count, freq_count, 2, seg_count, row_width)
    turned = jnp.stack([rows[:, :, 1], -rows[:, :, 0]], axis=2)
    left = jnp.concatenate([rows, turned], axis=4).reshape(
        time_count, freq_count, 2 * seg_count, 2 * row_width
    )
    norm_scale = 1.0 / math.sqrt(freq_count * seg_count * time_count)
    cross = jnp.einsum("tkqa,ctkqw->kcaw", left, every, preferred_element_type=jnp.float32)
    cross = (cross * norm_scale).astype(jnp.bfloat16)
    table = lag_table(freq_count, sample_count, LAGS)
    return lag_transform(cross, table)


def solution(mesh):
    return jax.shard_map(
        per_device,
        mesh=mesh,
        in_specs=(P("tm", "chan", None),),
        out_specs=P(("chan", "tm"), None, None),
        check_vma=False,
    )
```
